256 devices in a mesh: grp: 8 (over z), req: 4 (over x_hi, core), tp: 8 (over y, x_lo).
Axes of the slice: x: 4 (x_hi: 2, x_lo: 2; x = x_hi * 2 + x_lo), y: 4, z: 8, core: 2. Of those that a mesh axis runs over, the one named last changes fastest.
Arguments:
- stretch_in: bfloat16 [8, 2048, 3072], P('grp', 'req', 'tp'), may hold values from -48 to 48
- norm_gain: bfloat16 [3072], replicated, may hold values from 0.099609375 to 1.8984375
- w_qkv: bfloat16 [3072, 3, 3072], P(('grp', 'req'), None, 'tp'), may hold values from -1 to 1
- w_out: bfloat16 [3072, 3072], P('tp', ('grp', 'req')), may hold values from -0.625 to 0.625
- prompt_cache: bfloat16 [8, 2, 2, 1024, 3072], P('grp', None, None, 'req', 'tp'), may hold values from -6 to 6
- prompt_len: int32 [8], replicated, may hold values from 256 to 1024, as said below
- req_count: int32 [8], replicated, may hold values from 8 to 16, as said below
- req_map: int32 [8, 16], replicated, may hold values from -1 to 31, as said below
- prefix_len: int32 [8, 16], replicated, may hold values from 1 to 1024, as said below
- slot_query: bfloat16 [32, 8, 2, 3072], P(('grp', 'req'), None, None, 'tp'), may hold values from -8 to 8
- slot_new_kv: bfloat16 [32, 8, 2, 2, 3072], P(('grp', 'req'), None, None, None, 'tp'), may hold values from -6 to 6
Outputs:
- stretch_branch: bfloat16 [8, 2048, 3072], P('grp', 'req', 'tp')
- slot_out: bfloat16 [32, 8, 2, 3072], P(('grp', 'req'), None, None, 'tp')
The draws below stay inside these ranges and needn't reach their ends.
Inputs may be any that keep to these rules, and one draw needn't show every extreme that they name: `prompt_len`: some group's prompt fills all 1024 positions. prefix_len[g, r] <= prompt_len[g]; request 0 of every group attends to its whole prompt. `req_count`: some group has 16 requests. `req_map`: entries of requests that are not live are -1; every replica serves at most 8 live requests, and some replica exactly 8.
All inputs are finite; a program needn't handle non-finite values.
Results may differ from the reference program's by a relative error of at most 0.02.
Values may be sent and summed in bfloat16 or wider, within the bound.
No kernel may reach another device: no remote copies, remote signals or barrier semaphores. Data moves between devices by JAX's collectives and lax.ppermute only.
A program may use at most 128 MiB of HBM per device.

```python
import math
import jax
import jax.numpy as jnp
from jax import lax

D = 3072
HEADS = 32
HD = 96
CACHE = 1024
LAYERS_C = 2
RMAX = 16
SLOTS = 8
GROUPS = 8
REPLICAS = 32
STRETCH = 2048
HT = 4
N_TP = 8


def lengths_and_prefix(key):
    base_key = jax.random.fold_in(key, 101)
    key_len, key_top, key_pre = jax.random.split(base_key, 3)
    groups_iota = jnp.arange(GROUPS, dtype=jnp.int32)
    lengths = jax.random.randint(key_len, (GROUPS,), CACHE // 4, CACHE + 1)
    longest = jax.random.randint(key_top, (), 0, GROUPS)
    lengths = jnp.where(groups_iota == longest, CACHE, lengths)
    prefix = jax.random.randint(key_pre, (GROUPS, RMAX), 1, lengths[:, None] + 1)
    prefix = jnp.where(jnp.arange(RMAX, dtype=jnp.int32)[None, :] == 0, lengths[:, None], prefix)
    return (lengths.astype(jnp.int32), prefix.astype(jnp.int32))


def counts_and_map(key):
    base_key = jax.random.fold_in(key, 202)
    key_count, key_top, key_home, key_pool = jax.random.split(base_key, 4)
    groups_iota = jnp.arange(GROUPS, dtype=jnp.int32)
    counts = jax.random.randint(key_count, (GROUPS,), RMAX // 2, RMAX + 1)
    busiest = jax.random.randint(key_top, (), 0, GROUPS)
    counts = jnp.where(groups_iota == busiest, RMAX, jnp.where(groups_iota == (busiest + 1) % GROUPS, RMAX // 2, counts))
    flat_count = GROUPS * RMAX
    request_ids = jnp.arange(flat_count, dtype=jnp.int32)
    group_of = request_ids // RMAX
    within = request_ids % RMAX
    is_live = within < counts[group_of]
    forced = (group_of == busiest) & (within < SLOTS)
    order_key = jnp.where(forced, within, SLOTS + request_ids)
    sort_order = jnp.argsort(order_key)
    position = jnp.argsort(sort_order)
    home_replica = jax.random.randint(key_home, (), 0, REPLICAS)
    pool_size = (REPLICAS - 1) * SLOTS
    slot_pool = (home_replica + 1 + jnp.arange(pool_size, dtype=jnp.int32) // SLOTS) % REPLICAS
    slot_pool = jax.random.permutation(key_pool, slot_pool)
    pool_index = jnp.clip(position - SLOTS, 0, pool_size - 1)
    replica = jnp.where(position < SLOTS, home_replica, slot_pool[pool_index])
    mapping = jnp.where(is_live, replica, -1)
    return (counts.astype(jnp.int32), mapping.reshape(GROUPS, RMAX).astype(jnp.int32))


def draw_prompt_len(key, part):
    return lengths_and_prefix(key)[0]


def draw_prefix_len(key, part):
    return lengths_and_prefix(key)[1]


def draw_req_count(key, part):
    return counts_and_map(key)[0]


def draw_req_map(key, part):
    return counts_and_map(key)[1]


def draw_stretch_in(key, part):
    base_key = jax.random.fold_in(key, 404)
    key_base, key_row, key_col = jax.random.split(base_key, 3)
    full_shape = (GROUPS, STRETCH, D)
    row_scale = jnp.exp(jax.random.uniform(key_row, (GROUPS, STRETCH, 1), minval=math.log(0.3), maxval=math.log(3.0)))
    col_scale = jnp.exp(jax.random.uniform(key_col, (1, 1, D), minval=math.log(0.4), maxval=math.log(4.0)))
    values = jnp.clip(jax.random.normal(key_base, full_shape), -4.0, 4.0) * col_scale
    return (values * row_scale).astype(jnp.bfloat16)


def draw_w_qkv(key, part):
    base_key = jax.random.fold_in(key, 606)
    key_base = jax.random.fold_in(base_key, 0)
    full_shape = (D, 3, D)
    values = jnp.clip(jax.random.normal(key_base, full_shape), -4.0, 4.0) / math.sqrt(D)
    return values.astype(jnp.bfloat16)


def draw_prompt_cache(key, part):
    base_key = jax.random.fold_in(key, 707)
    key_base = jax.random.fold_in(base_key, 0)
    full_shape = (GROUPS, LAYERS_C, 2, CACHE, D)
    values = jnp.clip(jax.random.normal(key_base, full_shape), -4.0, 4.0)
    return values.astype(jnp.bfloat16)


def draw_slot_query(key, part):
    base_key = jax.random.fold_in(key, 808)
    key_base = jax.random.fold_in(base_key, 0)
    full_shape = (REPLICAS, SLOTS, LAYERS_C, D)
    values = jnp.clip(jax.random.normal(key_base, full_shape), -4.0, 4.0)
    return values.astype(jnp.bfloat16)


def levels(key, shape, cuts, smallest, top_value):
    def one(axis_at, parts):
        heights = jax.random.uniform(jax.random.fold_in(jax.random.fold_in(key, 6), axis_at), (parts,), jnp.float32, smallest / len(cuts), top_value / len(cuts))
        return jnp.repeat(jnp.exp(heights), shape[axis_at] // parts).reshape((-1,) + (1,) * (len(shape) - axis_at - 1))

    gain = one(*cuts[0])
    for cut in cuts[1:]:
        gain = gain * one(*cut)
    return gain


def gaussian(stream_key, shape, deviation, reach, shards=(), kind=jnp.bfloat16):
    values = deviation * jax.random.normal(stream_key, shape, jnp.float32)
    if shards:
        values = values * levels(stream_key, shape, shards, -0.22, 0.18)
    return jnp.clip(values, -reach, reach).astype(kind)


def setup_inputs(seed: int = 0) -> dict:
    splits = jax.random.split(jax.random.key(seed), 12)
    return {
        "stretch_in": draw_stretch_in(jax.random.fold_in(splits[11], 71), 0),
        "norm_gain": jnp.clip(1.0 + 0.18 * jax.random.normal(splits[1], (D,), jnp.float32), 0.099609375, 1.8984375).astype(jnp.bfloat16),
        "w_qkv": draw_w_qkv(jax.random.fold_in(splits[11], 71), 0),
        "w_out": gaussian(splits[3], (D, D), HD ** -0.5, 0.625, ((0, 8), (1, 32))),
        "prompt_cache": draw_prompt_cache(jax.random.fold_in(splits[11], 71), 0),
        "prompt_len": draw_prompt_len(jax.random.fold_in(splits[11], 71), 0),
        "req_count": draw_req_count(jax.random.fold_in(splits[11], 71), 0),
        "req_map": draw_req_map(jax.random.fold_in(splits[11], 71), 0),
        "prefix_len": draw_prefix_len(jax.random.fold_in(splits[11], 71), 0),
        "slot_query": draw_slot_query(jax.random.fold_in(splits[11], 71), 0),
        "slot_new_kv": gaussian(splits[10], (REPLICAS, SLOTS, LAYERS_C, 2, D), 1.0, 6.0, ((0, 32), (4, 8))),
    }


NEG_FLOOR = -1e+30
NORM_EPS = 1e-05
ROPE_BASE = 10000.0

def rope_angles(positions, head_size):
    half_size = head_size // 2
    freqs = ROPE_BASE ** (-(jnp.arange(half_size, dtype=jnp.float32) * 2.0 / head_size))
    angles = positions.astype(jnp.float32)[:, None] * freqs[None, :]
    return (jnp.cos(angles), jnp.sin(angles))

def rotate_pairs(values, cosine, sine_table):
    half_size = values.shape[-1] // 2
    first_half = values[..., :half_size]
    second_half = values[..., half_size:]
    cos_b = cosine[:, None, :]
    sin_b = sine_table[:, None, :]
    return jnp.concatenate([first_half * cos_b - second_half * sin_b, second_half * cos_b + first_half * sin_b], axis=-1)

def exact_round(values):
    return lax.optimization_barrier(values.astype(jnp.bfloat16)).astype(jnp.float32)

def stretch_group(group_rows, cache_group, length, norm_gain, w_qkv, w_out):
    scale_factor = HD ** (-0.5)
    widened = group_rows.astype(jnp.float32)
    mean_square = lax.optimization_barrier(jnp.mean(widened * widened, axis=1, keepdims=True))
    normed = (widened * lax.rsqrt(mean_square + NORM_EPS) * norm_gain.astype(jnp.float32)).astype(jnp.bfloat16)
    projected = jnp.dot(normed, w_qkv.reshape(D, 3 * D), preferred_element_type=jnp.float32).reshape(STRETCH, 3, HEADS, HD)
    positions = length + jnp.arange(STRETCH, dtype=jnp.int32)
    cosine, sine_table = rope_angles(positions, HD)
    queries = rotate_pairs(projected[:, 0], cosine, sine_table).astype(jnp.bfloat16)
    new_keys = rotate_pairs(projected[:, 1], cosine, sine_table).astype(jnp.bfloat16)
    new_values = projected[:, 2].astype(jnp.bfloat16)
    all_keys = jnp.concatenate([cache_group[0, 0].reshape(CACHE, HEADS, HD), new_keys], axis=0)
    all_values = jnp.concatenate([cache_group[0, 1].reshape(CACHE, HEADS, HD), new_values], axis=0)
    key_index = jnp.arange(CACHE + STRETCH, dtype=jnp.int32)
    query_index = jnp.arange(STRETCH, dtype=jnp.int32)
    allowed = jnp.where(key_index[None, :] < CACHE, key_index[None, :] < length, key_index[None, :] - CACHE <= query_index[:, None])

    def one_head(head_id):
        query_head = lax.dynamic_index_in_dim(queries, head_id, 1, keepdims=False)
        key_head = lax.dynamic_index_in_dim(all_keys, head_id, 1, keepdims=False)
        value_head = lax.dynamic_index_in_dim(all_values, head_id, 1, keepdims=False)
        scores = jnp.dot(query_head, key_head.T, preferred_element_type=jnp.float32) * scale_factor
        masked = jnp.where(allowed, scores, NEG_FLOOR)
        row_peak = lax.optimization_barrier(jnp.max(masked, axis=1, keepdims=True))
        weights = jnp.where(allowed, jnp.exp(masked - row_peak), 0.0)
        totals = lax.optimization_barrier(jnp.sum(weights, axis=1, keepdims=True))
        mixed = jnp.dot(weights.astype(jnp.bfloat16), value_head, preferred_element_type=jnp.float32)
        return (mixed / totals).astype(jnp.bfloat16)
    attended = lax.map(one_head, jnp.arange(HEADS, dtype=jnp.int32))
    attended = jnp.transpose(attended, (1, 0, 2)).reshape(STRETCH, D)
    block_width = HT * HD
    summed = jnp.zeros((STRETCH, D), jnp.float32)
    for block_index in range(N_TP):
        part_rows = attended[:, block_index * block_width:(block_index + 1) * block_width]
        part_weight = w_out[block_index * block_width:(block_index + 1) * block_width]
        product = jnp.dot(part_rows, part_weight, preferred_element_type=jnp.float32)
        summed = summed + exact_round(product)
    return summed.astype(jnp.bfloat16)

def reference(stretch_in, norm_gain, w_qkv, w_out, prompt_cache, prompt_len, req_count, req_map, prefix_len, slot_query, slot_new_kv):

    def per_group(items):
        group_rows, cache_group, length = items
        return stretch_group(group_rows, cache_group, length, norm_gain, w_qkv, w_out)
    stretch_branch = lax.map(per_group, (stretch_in, prompt_cache, prompt_len))
    flat_count = GROUPS * RMAX
    request_ids = jnp.arange(flat_count, dtype=jnp.int32)
    request_live = request_ids % RMAX < req_count[request_ids // RMAX]
    flat_map = req_map.reshape(flat_count)
    member = (flat_map[None, :] == jnp.arange(REPLICAS, dtype=jnp.int32)[:, None]) & request_live[None, :]
    order_rank = jnp.cumsum(member.astype(jnp.int32), axis=1) - 1
    slot_hit = member[:, None, :] & (order_rank[:, None, :] == jnp.arange(SLOTS, dtype=jnp.int32)[None, :, None])
    slot_request = lax.optimization_barrier(jnp.sum(jnp.where(slot_hit, request_ids[None, None, :], 0), axis=2)).reshape(REPLICAS * SLOTS)
    slot_alive = jnp.any(slot_hit, axis=2).reshape(REPLICAS * SLOTS)
    prefix_flat = prefix_len.reshape(flat_count)
    scale_factor = HD ** (-0.5)

    def decode_slot(items):
        request, is_alive, query_rows, new_rows = items
        group_id = request // RMAX
        prefix = prefix_flat[request]
        cache_group = lax.dynamic_index_in_dim(prompt_cache, group_id, 0, keepdims=False)
        cache_keys = cache_group[:, 0].reshape(LAYERS_C, CACHE, HEADS, HD).astype(jnp.float32)
        cache_values = cache_group[:, 1].reshape(LAYERS_C, CACHE, HEADS, HD).astype(jnp.float32)
        query_f = query_rows.reshape(LAYERS_C, HEADS, HD).astype(jnp.float32)
        own_key = new_rows[:, 0].reshape(LAYERS_C, HEADS, HD).astype(jnp.float32)
        own_value = new_rows[:, 1].reshape(LAYERS_C, HEADS, HD).astype(jnp.float32)
        scores = jnp.einsum('lhe,lphe->lhp', query_f, cache_keys, precision=lax.Precision.HIGHEST) * scale_factor
        allowed = (jnp.arange(CACHE, dtype=jnp.int32) < prefix)[None, None, :]
        own_score = lax.optimization_barrier(jnp.sum(query_f * own_key, axis=2)) * scale_factor
        masked = jnp.where(allowed, scores, NEG_FLOOR)
        row_peak = jnp.maximum(lax.optimization_barrier(jnp.max(masked, axis=2)), own_score)
        weights = jnp.where(allowed, jnp.exp(masked - row_peak[..., None]), 0.0)
        own_weight = jnp.exp(own_score - row_peak)
        totals = lax.optimization_barrier(jnp.sum(weights, axis=2)) + own_weight
        mixed = jnp.einsum('lhp,lphe->lhe', exact_round(weights), cache_values, precision=lax.Precision.HIGHEST)
        mixed = mixed + exact_round(own_weight)[..., None] * own_value
        result = mixed / totals[..., None]
        result = jnp.where(is_alive, result, 0.0)
        return result.reshape(LAYERS_C, D).astype(jnp.bfloat16)
    slot_out = lax.map(decode_slot, (slot_request, slot_alive, slot_query.reshape(REPLICAS * SLOTS, LAYERS_C, D), slot_new_kv.reshape(REPLICAS * SLOTS, LAYERS_C, 2, D)))
    return (stretch_branch, slot_out.reshape(REPLICAS, SLOTS, LAYERS_C, D))
```

```python
import jax
import jax.numpy as jnp
from jax import lax
from jax.sharding import PartitionSpec as P

HD = 96


NEG_FLOOR = -1e30
NORM_EPS = 1e-05
ROPE_BASE = 10000.0


def merged_2(value, axis, combine):
    everything = jax.tree.map(lambda part: lax.all_gather(part, axis), value)
    first = jax.tree.map(lambda part: part[0], everything)

    def turn(k, so_far):
        return combine(so_far, jax.tree.map(lambda part: part[k], everything))

    return lax.fori_loop(1, lax.axis_size(axis), turn, first)


def rope_angles(positions, head_size):
    half_size = head_size // 2
    freqs = ROPE_BASE ** (-(jnp.arange(half_size, dtype=jnp.float32) * 2.0 / head_size))
    angles = positions.astype(jnp.float32)[:, None] * freqs[None, :]
    return (jnp.cos(angles), jnp.sin(angles))


def rotate_pairs(values, cosine, sine_table):
    half_size = values.shape[-1] // 2
    first_half = values[..., :half_size]
    second_half = values[..., half_size:]
    cos_b = cosine[:, None, :]
    sin_b = sine_table[:, None, :]
    return jnp.concatenate(
        [first_half * cos_b - second_half * sin_b, second_half * cos_b + first_half * sin_b],
        axis=-1,
    )


def exact_round(values):
    return lax.optimization_barrier(values.astype(jnp.bfloat16)).astype(jnp.float32)


def merge_soft(first_state, second_state):
    peak_one, total_one, accum_one = first_state
    peak_two, total_two, accum_two = second_state
    peak_new = jnp.maximum(peak_one, peak_two)
    factor_one = jnp.exp(peak_one - peak_new)
    factor_two = jnp.exp(peak_two - peak_new)
    return (
        peak_new,
        total_one * factor_one + total_two * factor_two,
        accum_one * factor_one[..., None] + accum_two * factor_two[..., None],
    )


def cache_partial(queries, cache_keys, cache_values, allowed, scale_factor):
    scores = (
        jnp.einsum("slhe,lkhe->slhk", queries, cache_keys, preferred_element_type=jnp.float32)
        * scale_factor
    )
    key_gate = allowed[:, None, None, :]
    masked = jnp.where(key_gate, scores, NEG_FLOOR)
    row_peak = jnp.max(masked, axis=3)
    weights = jnp.where(key_gate, jnp.exp(masked - row_peak[..., None]), 0.0)
    totals = jnp.sum(weights, axis=3)
    accumulated = jnp.einsum(
        "slhk,lkhe->slhe",
        weights.astype(jnp.bfloat16),
        cache_values,
        preferred_element_type=jnp.float32,
    )
    return (row_peak, totals, accumulated)


def finish_slots(merged, own_query, own_kv, own_alive, scale_factor):
    row_peak, totals, accumulated = merged
    own_key = own_kv[:, :, 0]
    own_value = own_kv[:, :, 1]
    own_score = (
        jnp.einsum("slhe,slhe->slh", own_query, own_key, preferred_element_type=jnp.float32)
        * scale_factor
    )
    new_peak = jnp.maximum(row_peak, own_score)
    shrink = jnp.exp(row_peak - new_peak)
    own_weight = jnp.exp(own_score - new_peak)
    new_total = totals * shrink + own_weight
    mixed = accumulated * shrink[..., None] + exact_round(own_weight)[..., None] * own_value.astype(
        jnp.float32
    )
    result = mixed / new_total[..., None]
    result = jnp.where(own_alive[:, None, None, None], result, 0.0)
    return result.astype(jnp.bfloat16)


def per_device(
    stretch_in,
    norm_gain,
    w_qkv,
    w_out,
    prompt_cache,
    prompt_len,
    req_count,
    req_map,
    prefix_len,
    slot_query,
    slot_new_kv,
):
    group_id = lax.axis_index("grp")
    block_id = lax.axis_index("req")
    replica_id = lax.axis_index(("grp", "req"))
    replicas = lax.axis_size(("grp", "req"))
    stretch_rows = stretch_in.shape[1]
    tensor_width = stretch_in.shape[2]
    head_size = HD
    local_heads = tensor_width // head_size
    cache_rows = prompt_cache.shape[3]
    layer_count = prompt_cache.shape[1]
    scale_factor = head_size ** (-0.5)
    length = lax.dynamic_index_in_dim(prompt_len, group_id, 0, keepdims=False)
    full_rows = lax.all_gather(stretch_in[0], "tp", axis=1, tiled=True)
    widened = full_rows.astype(jnp.float32)
    mean_square = jnp.mean(widened * widened, axis=1, keepdims=True)
    normed = (widened * lax.rsqrt(mean_square + NORM_EPS) * norm_gain.astype(jnp.float32)).astype(
        jnp.bfloat16
    )
    weight_piece = lax.all_gather(w_qkv, ("grp", "req"), axis=0, tiled=True)
    projected = jnp.dot(
        normed, weight_piece.reshape(weight_piece.shape[0], -1), preferred_element_type=jnp.float32
    )
    projected = projected.reshape(stretch_rows, 3, local_heads, head_size)
    query_pos = block_id * stretch_rows + jnp.arange(stretch_rows, dtype=jnp.int32)
    cosine, sine_table = rope_angles(length + query_pos, head_size)
    queries = rotate_pairs(projected[:, 0], cosine, sine_table).astype(jnp.bfloat16)
    new_keys = rotate_pairs(projected[:, 1], cosine, sine_table).astype(jnp.bfloat16)
    new_values = projected[:, 2].astype(jnp.bfloat16)
    fresh_kv = jnp.stack(
        [
            new_keys.reshape(stretch_rows, tensor_width),
            new_values.reshape(stretch_rows, tensor_width),
        ],
        axis=0,
    )
    local_kv = jnp.concatenate([prompt_cache[0, 0], fresh_kv], axis=1)
    block_span = cache_rows + stretch_rows

    def attend_rows(carry, kv_piece, first_row):
        row_peak, totals, accumulated = carry
        piece_rows = kv_piece.shape[1]
        row_index = first_row + jnp.arange(piece_rows, dtype=jnp.int32)
        shard_index = row_index // block_span
        offset = row_index % block_span
        from_cache = offset < cache_rows
        cache_pos = shard_index * cache_rows + offset
        stretch_pos = shard_index * stretch_rows + offset - cache_rows
        allowed = jnp.where(
            from_cache[None, :],
            cache_pos[None, :] < length,
            stretch_pos[None, :] <= query_pos[:, None],
        )
        piece_keys = kv_piece[0].reshape(piece_rows, local_heads, head_size)
        piece_values = kv_piece[1].reshape(piece_rows, local_heads, head_size)
        scores = (
            jnp.einsum("qhe,khe->hqk", queries, piece_keys, preferred_element_type=jnp.float32)
            * scale_factor
        )
        key_gate = allowed[None]
        masked = jnp.where(key_gate, scores, NEG_FLOOR)
        new_peak = jnp.maximum(row_peak, jnp.max(masked, axis=2))
        shrink = jnp.exp(row_peak - new_peak)
        weights = jnp.where(key_gate, jnp.exp(masked - new_peak[..., None]), 0.0)
        totals = totals * shrink + jnp.sum(weights, axis=2)
        update = jnp.einsum(
            "hqk,khe->qhe",
            weights.astype(jnp.bfloat16),
            piece_values,
            preferred_element_type=jnp.float32,
        )
        accumulated = accumulated * jnp.transpose(shrink)[:, :, None] + update
        return (new_peak, totals, accumulated)

    start_state = (
        jnp.full((local_heads, stretch_rows), NEG_FLOOR, jnp.float32),
        jnp.zeros((local_heads, stretch_rows), jnp.float32),
        jnp.zeros((stretch_rows, local_heads, head_size), jnp.float32),
    )
    kv_piece = lax.all_gather(local_kv, "req", axis=1, tiled=True)
    piece_rows = kv_piece.shape[1]

    def one_block(block_step, inner_state):
        part_kv = lax.dynamic_slice_in_dim(kv_piece, block_step * block_span, block_span, 1)
        return attend_rows(inner_state, part_kv, block_step * block_span)

    row_peak, totals, accumulated = lax.fori_loop(
        0, piece_rows // block_span, one_block, start_state
    )
    attended = (
        (accumulated / jnp.transpose(totals)[:, :, None])
        .astype(jnp.bfloat16)
        .reshape(stretch_rows, tensor_width)
    )
    out_weight_t = lax.all_gather(jnp.transpose(w_out), ("grp", "req"), axis=0, tiled=True)
    partial_sum = lax.dot_general(
        attended,
        out_weight_t,
        (((1,), (1,)), ((), ())),
        preferred_element_type=jnp.float32,
    ).astype(jnp.bfloat16)
    branch = lax.psum_scatter(
        partial_sum.astype(jnp.float32).astype(jnp.bfloat16), "tp", scatter_dimension=1, tiled=True
    )
    group_total, max_requests = req_map.shape
    flat_count = group_total * max_requests
    slot_count = slot_query.shape[1]
    request_ids = jnp.arange(flat_count, dtype=jnp.int32)
    group_of = request_ids // max_requests
    count_of = jnp.sum(
        jnp.where(
            group_of[:, None] == jnp.arange(group_total, dtype=jnp.int32)[None, :],
            req_count[None, :],
            0,
        ),
        axis=1,
    )
    request_live = request_ids % max_requests < count_of
    flat_map = req_map.reshape(flat_count)
    earlier = (
        (flat_map[None, :] == flat_map[:, None])
        & request_live[None, :]
        & (request_ids[None, :] < request_ids[:, None])
    )
    order_rank = jnp.sum(earlier.astype(jnp.int32), axis=1)
    slot_of = jnp.where(request_live, flat_map * slot_count + order_rank, 0)
    prefix_flat = prefix_len.reshape(flat_count)
    first_request = group_id * max_requests
    mine_live = lax.dynamic_slice_in_dim(request_live, first_request, max_requests, 0)
    mine_slot = lax.dynamic_slice_in_dim(slot_of, first_request, max_requests, 0)
    mine_prefix = lax.dynamic_slice_in_dim(prefix_flat, first_request, max_requests, 0)
    all_queries = lax.all_gather(
        slot_query[0].reshape(slot_count, layer_count * tensor_width), ("grp", "req"), axis=0, tiled=True
    )
    picked = jnp.take(all_queries, mine_slot, axis=0).reshape(
        max_requests, layer_count, local_heads, head_size
    )
    cache_keys = prompt_cache[0, :, 0].reshape(layer_count, cache_rows, local_heads, head_size)
    cache_values = prompt_cache[0, :, 1].reshape(layer_count, cache_rows, local_heads, head_size)
    cache_pos = block_id * cache_rows + jnp.arange(cache_rows, dtype=jnp.int32)
    allowed = mine_live[:, None] & (cache_pos[None, :] < mine_prefix[:, None])
    part_peak, part_total, part_accum = cache_partial(
        picked, cache_keys, cache_values, allowed, scale_factor
    )
    packed = jnp.concatenate([part_peak[..., None], part_total[..., None], part_accum], axis=-1)
    block_parts = lax.all_gather(packed, "req", axis=0)
    peaks = block_parts[..., 0]
    group_peak = jnp.max(peaks, axis=0)
    factor = jnp.exp(peaks - group_peak[None])
    group_total_w = jnp.sum(block_parts[..., 1] * factor, axis=0)
    group_accum = jnp.sum(block_parts[..., 2:] * factor[..., None], axis=0)
    merged_group = jnp.concatenate(
        [group_peak[..., None], group_total_w[..., None], group_accum], axis=-1
    )
    every_group = lax.all_gather(merged_group, "grp", axis=0, tiled=True)
    slot_hit = (
        request_live[None, :]
        & (flat_map[None, :] == replica_id)
        & (order_rank[None, :] == jnp.arange(slot_count, dtype=jnp.int32)[:, None])
    )
    own_request = jnp.sum(jnp.where(slot_hit, request_ids[None, :], 0), axis=1)
    own_alive = jnp.any(slot_hit, axis=1)
    own_state = jnp.take(every_group, own_request, axis=0)
    merged = (own_state[..., 0], own_state[..., 1], own_state[..., 2:])
    own_query = slot_query[0].reshape(slot_count, layer_count, local_heads, head_size)
    own_kv = slot_new_kv[0].reshape(slot_count, layer_count, 2, local_heads, head_size)
    result = finish_slots(merged, own_query, own_kv, own_alive, scale_factor)
    return (branch[None], result.reshape(slot_count, layer_count, tensor_width)[None])


def solution(mesh):
    placed = (
        P("grp", "req", "tp"),
        P(),
        P(("grp", "req"), None, "tp"),
        P("tp", ("grp", "req")),
        P("grp", None, None, "req", "tp"),
        P(),
        P(),
        P(),
        P(),
        P(("grp", "req"), None, None, "tp"),
        P(("grp", "req"), None, None, None, "tp"),
    )
    return jax.shard_map(
        per_device,
        mesh=mesh,
        in_specs=placed,
        out_specs=(P("grp", "req", "tp"), P(("grp", "req"), None, None, "tp")),
        check_vma=False,
    )
```

```python
import jax
import jax.numpy as jnp
from jax import lax
from jax.sharding import PartitionSpec as P

HD = 96


NEG_FLOOR = -1e30
NORM_EPS = 1e-05
ROPE_BASE = 10000.0


def rope_angles(positions, head_size):
    half_size = head_size // 2
    freqs = ROPE_BASE ** (-(jnp.arange(half_size, dtype=jnp.float32) * 2.0 / head_size))
    angles = positions.astype(jnp.float32)[:, None] * freqs[None, :]
    return (jnp.cos(angles), jnp.sin(angles))


def rotate_pairs(values, cosine, sine_table):
    half_size = values.shape[-1] // 2
    first_half = values[..., :half_size]
    second_half = values[..., half_size:]
    cos_b = cosine[:, None, :]
    sin_b = sine_table[:, None, :]
    return jnp.concatenate(
        [first_half * cos_b - second_half * sin_b, second_half * cos_b + first_half * sin_b],
        axis=-1,
    )


def exact_round(values):
    return lax.optimization_barrier(values.astype(jnp.bfloat16)).astype(jnp.float32)


def cache_partial(queries, cache_keys, cache_values, allowed, scale_factor):
    scores = (
        jnp.einsum("slhe,lkhe->slhk", queries, cache_keys, preferred_element_type=jnp.float32)
        * scale_factor
    )
    key_gate = allowed[:, None, None, :]
    masked = jnp.where(key_gate, scores, NEG_FLOOR)
    row_peak = jnp.max(masked, axis=3)
    weights = jnp.where(key_gate, jnp.exp(masked - row_peak[..., None]), 0.0)
    totals = jnp.sum(weights, axis=3)
    accumulated = jnp.einsum(
        "slhk,lkhe->slhe",
        weights.astype(jnp.bfloat16),
        cache_values,
        preferred_element_type=jnp.float32,
    )
    return (row_peak, totals, accumulated)


def finish_slots(merged, own_query, own_kv, own_alive, scale_factor):
    row_peak, totals, accumulated = merged
    own_key = own_kv[:, :, 0]
    own_value = own_kv[:, :, 1]
    own_score = (
        jnp.einsum("slhe,slhe->slh", own_query, own_key, preferred_element_type=jnp.float32)
        * scale_factor
    )
    new_peak = jnp.maximum(row_peak, own_score)
    shrink = jnp.exp(row_peak - new_peak)
    own_weight = jnp.exp(own_score - new_peak)
    new_total = totals * shrink + own_weight
    mixed = accumulated * shrink[..., None] + exact_round(own_weight)[..., None] * own_value.astype(
        jnp.float32
    )
    result = mixed / new_total[..., None]
    result = jnp.where(own_alive[:, None, None, None], result, 0.0)
    return result.astype(jnp.bfloat16)


def gather_shifts(value, axis, count):
    pieces = [value]
    for shift in range(1, count):
        pieces.append(
            lax.ppermute(value, axis, [(i, (i + shift) % count) for i in range(count)])
        )
    return pieces


def per_device(
    stretch_in,
    norm_gain,
    w_qkv,
    w_out,
    prompt_cache,
    prompt_len,
    req_count,
    req_map,
    prefix_len,
    slot_query,
    slot_new_kv,
):
    group_id = lax.axis_index("grp")
    block_id = lax.axis_index("req")
    tensor_id = lax.axis_index("tp")
    replica_id = lax.axis_index(("grp", "req"))
    n_tp = lax.axis_size("tp")
    n_req = lax.axis_size("req")
    n_grp = lax.axis_size("grp")
    stretch_rows = stretch_in.shape[1]
    local_width = stretch_in.shape[2]
    tensor_width = local_width * n_tp
    head_size = HD
    local_heads = local_width // head_size
    cache_rows = prompt_cache.shape[3]
    layer_count = prompt_cache.shape[1]
    slot_count = slot_query.shape[1]
    scale_factor = head_size ** (-0.5)
    length = lax.dynamic_index_in_dim(prompt_len, group_id, 0, keepdims=False)

    rows_in = stretch_in[0]
    row_pieces = gather_shifts(rows_in, "tp", n_tp)
    full_rows = jnp.zeros((stretch_rows, tensor_width), rows_in.dtype)
    for shift, piece in enumerate(row_pieces):
        source = (tensor_id - shift) % n_tp
        full_rows = lax.dynamic_update_slice_in_dim(full_rows, piece, source * local_width, 1)
    widened = full_rows.astype(jnp.float32)
    mean_square = jnp.mean(widened * widened, axis=1, keepdims=True)
    normed = (widened * lax.rsqrt(mean_square + NORM_EPS) * norm_gain.astype(jnp.float32)).astype(
        jnp.bfloat16
    )

    weight_rows = w_qkv.shape[0]
    weight_cols = w_qkv.shape[1] * w_qkv.shape[2]
    query_len = slot_count * layer_count * local_width
    query_rows = -(-query_len // weight_cols)
    query_flat = jnp.pad(
        slot_query[0].reshape(query_len), (0, query_rows * weight_cols - query_len)
    ).reshape(query_rows, weight_cols)
    combo = jnp.concatenate([w_qkv.reshape(weight_rows, weight_cols), query_flat], axis=0)
    gathered = lax.all_gather(combo, ("grp", "req"), axis=0)
    weight_piece = gathered[:, :weight_rows].reshape(-1, weight_cols)
    all_queries = (
        gathered[:, weight_rows:]
        .reshape(gathered.shape[0], query_rows * weight_cols)[:, :query_len]
        .reshape(gathered.shape[0] * slot_count, layer_count * local_width)
    )

    projected = jnp.dot(normed, weight_piece, preferred_element_type=jnp.float32)
    projected = projected.reshape(stretch_rows, 3, local_heads, head_size)
    query_pos = block_id * stretch_rows + jnp.arange(stretch_rows, dtype=jnp.int32)
    cosine, sine_table = rope_angles(length + query_pos, head_size)
    queries = rotate_pairs(projected[:, 0], cosine, sine_table).astype(jnp.bfloat16)
    new_keys = rotate_pairs(projected[:, 1], cosine, sine_table).astype(jnp.bfloat16)
    new_values = projected[:, 2].astype(jnp.bfloat16)
    fresh_kv = jnp.stack(
        [
            new_keys.reshape(stretch_rows, local_width),
            new_values.reshape(stretch_rows, local_width),
        ],
        axis=0,
    )
    local_kv = jnp.concatenate([prompt_cache[0, 0], fresh_kv], axis=1)
    block_span = cache_rows + stretch_rows

    def attend_rows(carry, kv_piece, source):
        row_peak, totals, accumulated = carry
        piece_rows = kv_piece.shape[1]
        offset = jnp.arange(piece_rows, dtype=jnp.int32)
        from_cache = offset < cache_rows
        cache_pos = source * cache_rows + offset
        stretch_pos = source * stretch_rows + offset - cache_rows
        allowed = jnp.where(
            from_cache[None, :],
            cache_pos[None, :] < length,
            stretch_pos[None, :] <= query_pos[:, None],
        )
        piece_keys = kv_piece[0].reshape(piece_rows, local_heads, head_size)
        piece_values = kv_piece[1].reshape(piece_rows, local_heads, head_size)
        scores = (
            jnp.einsum("qhe,khe->hqk", queries, piece_keys, preferred_element_type=jnp.float32)
            * scale_factor
        )
        key_gate = allowed[None]
        masked = jnp.where(key_gate, scores, NEG_FLOOR)
        new_peak = jnp.maximum(row_peak, jnp.max(masked, axis=2))
        shrink = jnp.exp(row_peak - new_peak)
        weights = jnp.where(key_gate, jnp.exp(masked - new_peak[..., None]), 0.0)
        totals = totals * shrink + jnp.sum(weights, axis=2)
        update = jnp.einsum(
            "hqk,khe->qhe",
            weights.astype(jnp.bfloat16),
            piece_values,
            preferred_element_type=jnp.float32,
        )
        accumulated = accumulated * jnp.transpose(shrink)[:, :, None] + update
        return (new_peak, totals, accumulated)

    state = (
        jnp.full((local_heads, stretch_rows), NEG_FLOOR, jnp.float32),
        jnp.zeros((local_heads, stretch_rows), jnp.float32),
        jnp.zeros((stretch_rows, local_heads, head_size), jnp.float32),
    )
    for shift, kv_piece in enumerate(gather_shifts(local_kv, "req", n_req)):
        state = attend_rows(state, kv_piece, (block_id - shift) % n_req)
    row_peak, totals, accumulated = state
    attended = (
        (accumulated / jnp.transpose(totals)[:, :, None])
        .astype(jnp.bfloat16)
        .reshape(stretch_rows, local_width)
    )
    out_weight_t = lax.all_gather(jnp.transpose(w_out), ("grp", "req"), axis=0, tiled=True)
    branch = None
    for shift in range(n_tp):
        target = (tensor_id + shift) % n_tp
        weight_block = lax.dynamic_slice_in_dim(out_weight_t, target * local_width, local_width, 0)
        product = lax.dot_general(
            attended,
            weight_block,
            (((1,), (1,)), ((), ())),
            preferred_element_type=jnp.float32,
        ).astype(jnp.bfloat16)
        if shift:
            product = lax.ppermute(
                product, "tp", [(i, (i + shift) % n_tp) for i in range(n_tp)]
            )
        term = product.astype(jnp.float32)
        branch = term if branch is None else branch + term
    branch = branch.astype(jnp.bfloat16)

    group_total, max_requests = req_map.shape
    flat_count = group_total * max_requests
    request_ids = jnp.arange(flat_count, dtype=jnp.int32)
    group_of = request_ids // max_requests
    count_of = jnp.sum(
        jnp.where(
            group_of[:, None] == jnp.arange(group_total, dtype=jnp.int32)[None, :],
            req_count[None, :],
            0,
        ),
        axis=1,
    )
    request_live = request_ids % max_requests < count_of
    flat_map = req_map.reshape(flat_count)
    earlier = (
        (flat_map[None, :] == flat_map[:, None])
        & request_live[None, :]
        & (request_ids[None, :] < request_ids[:, None])
    )
    order_rank = jnp.sum(earlier.astype(jnp.int32), axis=1)
    slot_of = jnp.where(request_live, flat_map * slot_count + order_rank, 0)
    prefix_flat = prefix_len.reshape(flat_count)
    first_request = group_id * max_requests
    mine_live = lax.dynamic_slice_in_dim(request_live, first_request, max_requests, 0)
    mine_slot = lax.dynamic_slice_in_dim(slot_of, first_request, max_requests, 0)
    mine_prefix = lax.dynamic_slice_in_dim(prefix_flat, first_request, max_requests, 0)
    picked = jnp.take(all_queries, mine_slot, axis=0).reshape(
        max_requests, layer_count, local_heads, head_size
    )
    cache_keys = prompt_cache[0, :, 0].reshape(layer_count, cache_rows, local_heads, head_size)
    cache_values = prompt_cache[0, :, 1].reshape(layer_count, cache_rows, local_heads, head_size)
    cache_pos = block_id * cache_rows + jnp.arange(cache_rows, dtype=jnp.int32)
    allowed = mine_live[:, None] & (cache_pos[None, :] < mine_prefix[:, None])
    part_peak, part_total, part_accum = cache_partial(
        picked, cache_keys, cache_values, allowed, scale_factor
    )
    packed = jnp.concatenate([part_peak[..., None], part_total[..., None], part_accum], axis=-1)
    block_parts = jnp.stack(gather_shifts(packed, "req", n_req), axis=0)
    peaks = block_parts[..., 0]
    group_peak = jnp.max(peaks, axis=0)
    factor = jnp.exp(peaks - group_peak[None])
    group_total_w = jnp.sum(block_parts[..., 1] * factor, axis=0)
    group_accum = jnp.sum(block_parts[..., 2:] * factor[..., None], axis=0)
    merged_group = jnp.concatenate(
        [group_peak[..., None], group_total_w[..., None], group_accum], axis=-1
    )
    every_group = jnp.concatenate(gather_shifts(merged_group, "grp", n_grp), axis=0)
    slot_hit = (
        request_live[None, :]
        & (flat_map[None, :] == replica_id)
        & (order_rank[None, :] == jnp.arange(slot_count, dtype=jnp.int32)[:, None])
    )
    own_request = jnp.sum(jnp.where(slot_hit, request_ids[None, :], 0), axis=1)
    own_alive = jnp.any(slot_hit, axis=1)
    home_shift = (group_id - own_request // max_requests) % n_grp
    own_state = jnp.take(
        every_group, home_shift * max_requests + own_request % max_requests, axis=0
    )
    merged = (own_state[..., 0], own_state[..., 1], own_state[..., 2:])
    own_query = slot_query[0].reshape(slot_count, layer_count, local_heads, head_size)
    own_kv = slot_new_kv[0].reshape(slot_count, layer_count, 2, local_heads, head_size)
    result = finish_slots(merged, own_query, own_kv, own_alive, scale_factor)
    return (branch[None], result.reshape(slot_count, layer_count, local_width)[None])


def solution(mesh):
    placed = (
        P("grp", "req", "tp"),
        P(),
        P(("grp", "req"), None, "tp"),
        P("tp", ("grp", "req")),
        P("grp", None, None, "req", "tp"),
        P(),
        P(),
        P(),
        P(),
        P(("grp", "req"), None, None, "tp"),
        P(("grp", "req"), None, None, None, "tp"),
    )
    return jax.shard_map(
        per_device,
        mesh=mesh,
        in_specs=placed,
        out_specs=(P("grp", "req", "tp"), P(("grp", "req"), None, None, "tp")),
        check_vma=False,
    )
```

```python
import jax
import jax.numpy as jnp
from jax import lax
from jax.sharding import PartitionSpec as P

HD = 96


NEG_FLOOR = -1e30
NORM_EPS = 1e-05
ROPE_BASE = 10000.0


def rope_angles(positions, head_size):
    half_size = head_size // 2
    freqs = ROPE_BASE ** (-(jnp.arange(half_size, dtype=jnp.float32) * 2.0 / head_size))
    angles = positions.astype(jnp.float32)[:, None] * freqs[None, :]
    return (jnp.cos(angles), jnp.sin(angles))


def rotate_pairs(values, cosine, sine_table):
    half_size = values.shape[-1] // 2
    first_half = values[..., :half_size]
    second_half = values[..., half_size:]
    cos_b = cosine[:, None, :]
    sin_b = sine_table[:, None, :]
    return jnp.concatenate(
        [first_half * cos_b - second_half * sin_b, second_half * cos_b + first_half * sin_b],
        axis=-1,
    )


def exact_round(values):
    return lax.optimization_barrier(values.astype(jnp.bfloat16)).astype(jnp.float32)


def cache_partial(queries, cache_keys, cache_values, allowed, scale_factor):
    scores = (
        jnp.einsum("slhe,lkhe->slhk", queries, cache_keys, preferred_element_type=jnp.float32)
        * scale_factor
    )
    key_gate = allowed[:, None, None, :]
    masked = jnp.where(key_gate, scores, NEG_FLOOR)
    row_peak = jnp.max(masked, axis=3)
    weights = jnp.where(key_gate, jnp.exp(masked - row_peak[..., None]), 0.0)
    totals = jnp.sum(weights, axis=3)
    accumulated = jnp.einsum(
        "slhk,lkhe->slhe",
        weights.astype(jnp.bfloat16),
        cache_values,
        preferred_element_type=jnp.float32,
    )
    return (row_peak, totals, accumulated)


def finish_slots(merged, own_query, own_kv, own_alive, scale_factor):
    row_peak, totals, accumulated = merged
    own_key = own_kv[:, :, 0]
    own_value = own_kv[:, :, 1]
    own_score = (
        jnp.einsum("slhe,slhe->slh", own_query, own_key, preferred_element_type=jnp.float32)
        * scale_factor
    )
    new_peak = jnp.maximum(row_peak, own_score)
    shrink = jnp.exp(row_peak - new_peak)
    own_weight = jnp.exp(own_score - new_peak)
    new_total = totals * shrink + own_weight
    mixed = accumulated * shrink[..., None] + exact_round(own_weight)[..., None] * own_value.astype(
        jnp.float32
    )
    result = mixed / new_total[..., None]
    result = jnp.where(own_alive[:, None, None, None], result, 0.0)
    return result.astype(jnp.bfloat16)


def gather_shifts(value, axis, count):
    pieces = [value]
    for shift in range(1, count):
        pieces.append(
            lax.ppermute(value, axis, [(i, (i + shift) % count) for i in range(count)])
        )
    return pieces


def decode_slots(
    block_id, group_id, replica_id, n_req, n_grp, local_heads, head_size, scale_factor,
    prompt_cache, req_count, req_map, prefix_len, slot_query, slot_new_kv,
):
    cache_rows = prompt_cache.shape[3]
    layer_count = prompt_cache.shape[1]
    slot_count = slot_query.shape[1]
    group_total, max_requests = req_map.shape
    flat_count = group_total * max_requests
    request_ids = jnp.arange(flat_count, dtype=jnp.int32)
    group_of = request_ids // max_requests
    count_of = jnp.sum(
        jnp.where(
            group_of[:, None] == jnp.arange(group_total, dtype=jnp.int32)[None, :],
            req_count[None, :],
            0,
        ),
        axis=1,
    )
    request_live = request_ids % max_requests < count_of
    flat_map = req_map.reshape(flat_count)
    earlier = (
        (flat_map[None, :] == flat_map[:, None])
        & request_live[None, :]
        & (request_ids[None, :] < request_ids[:, None])
    )
    order_rank = jnp.sum(earlier.astype(jnp.int32), axis=1)
    slot_of = jnp.where(request_live, flat_map * slot_count + order_rank, 0)
    prefix_flat = prefix_len.reshape(flat_count)
    first_request = group_id * max_requests
    mine_live = lax.dynamic_slice_in_dim(request_live, first_request, max_requests, 0)
    mine_slot = lax.dynamic_slice_in_dim(slot_of, first_request, max_requests, 0)
    mine_prefix = lax.dynamic_slice_in_dim(prefix_flat, first_request, max_requests, 0)
    by_block = jnp.concatenate(gather_shifts(slot_query[0], "req", n_req), axis=0)
    all_queries = jnp.concatenate(gather_shifts(by_block, "grp", n_grp), axis=0)
    home_replica = mine_slot // slot_count
    query_row = (
        ((group_id - home_replica // n_req) % n_grp) * (n_req * slot_count)
        + ((block_id - home_replica % n_req) % n_req) * slot_count
        + mine_slot % slot_count
    )
    picked = jnp.take(all_queries, query_row, axis=0).reshape(
        max_requests, layer_count, local_heads, head_size
    )
    cache_keys = prompt_cache[0, :, 0].reshape(layer_count, cache_rows, local_heads, head_size)
    cache_values = prompt_cache[0, :, 1].reshape(layer_count, cache_rows, local_heads, head_size)
    cache_pos = block_id * cache_rows + jnp.arange(cache_rows, dtype=jnp.int32)
    allowed = mine_live[:, None] & (cache_pos[None, :] < mine_prefix[:, None])
    part_peak, part_total, part_accum = cache_partial(
        picked, cache_keys, cache_values, allowed, scale_factor
    )
    packed = jnp.concatenate([part_peak[..., None], part_total[..., None], part_accum], axis=-1)
    block_parts = jnp.stack(gather_shifts(packed, "req", n_req), axis=0)
    peaks = block_parts[..., 0]
    group_peak = jnp.max(peaks, axis=0)
    factor = jnp.exp(peaks - group_peak[None])
    group_total_w = jnp.sum(block_parts[..., 1] * factor, axis=0)
    group_accum = jnp.sum(block_parts[..., 2:] * factor[..., None], axis=0)
    merged_group = jnp.concatenate(
        [group_peak[..., None], group_total_w[..., None], group_accum], axis=-1
    )
    every_group = jnp.concatenate(gather_shifts(merged_group, "grp", n_grp), axis=0)
    slot_hit = (
        request_live[None, :]
        & (flat_map[None, :] == replica_id)
        & (order_rank[None, :] == jnp.arange(slot_count, dtype=jnp.int32)[:, None])
    )
    own_request = jnp.sum(jnp.where(slot_hit, request_ids[None, :], 0), axis=1)
    own_alive = jnp.any(slot_hit, axis=1)
    home_shift = (group_id - own_request // max_requests) % n_grp
    own_state = jnp.take(
        every_group, home_shift * max_requests + own_request % max_requests, axis=0
    )
    merged = (own_state[..., 0], own_state[..., 1], own_state[..., 2:])
    own_query = slot_query[0].reshape(slot_count, layer_count, local_heads, head_size)
    own_kv = slot_new_kv[0].reshape(slot_count, layer_count, 2, local_heads, head_size)
    result = finish_slots(merged, own_query, own_kv, own_alive, scale_factor)
    return result.reshape(slot_count, layer_count, local_heads * head_size)


def per_device(
    stretch_in,
    norm_gain,
    w_qkv,
    w_out,
    prompt_cache,
    prompt_len,
    req_count,
    req_map,
    prefix_len,
    slot_query,
    slot_new_kv,
):
    group_id = lax.axis_index("grp")
    block_id = lax.axis_index("req")
    tensor_id = lax.axis_index("tp")
    replica_id = lax.axis_index(("grp", "req"))
    n_tp = lax.axis_size("tp")
    n_req = lax.axis_size("req")
    n_grp = lax.axis_size("grp")
    stretch_rows = stretch_in.shape[1]
    local_width = stretch_in.shape[2]
    tensor_width = local_width * n_tp
    head_size = HD
    local_heads = local_width // head_size
    cache_rows = prompt_cache.shape[3]
    layer_count = prompt_cache.shape[1]
    slot_count = slot_query.shape[1]
    scale_factor = head_size ** (-0.5)
    length = lax.dynamic_index_in_dim(prompt_len, group_id, 0, keepdims=False)

    rows_in = stretch_in[0]
    row_pieces = gather_shifts(rows_in, "tp", n_tp)
    full_rows = jnp.zeros((stretch_rows, tensor_width), rows_in.dtype)
    for shift, piece in enumerate(row_pieces):
        source = (tensor_id - shift) % n_tp
        full_rows = lax.dynamic_update_slice_in_dim(full_rows, piece, source * local_width, 1)
    widened = full_rows.astype(jnp.float32)
    mean_square = jnp.mean(widened * widened, axis=1, keepdims=True)
    normed = (widened * lax.rsqrt(mean_square + NORM_EPS) * norm_gain.astype(jnp.float32)).astype(
        jnp.bfloat16
    )

    weight_piece = lax.all_gather(w_qkv, ("grp", "req"), axis=0, tiled=True)
    weight_piece = weight_piece.reshape(weight_piece.shape[0], -1)
    result = decode_slots(
        block_id, group_id, replica_id, n_req, n_grp, local_heads, head_size, scale_factor,
        prompt_cache, req_count, req_map, prefix_len, slot_query, slot_new_kv,
    )
    normed, result = lax.optimization_barrier((normed, result))

    projected = jnp.dot(normed, weight_piece, preferred_element_type=jnp.float32)
    projected = projected.reshape(stretch_rows, 3, local_heads, head_size)
    query_pos = block_id * stretch_rows + jnp.arange(stretch_rows, dtype=jnp.int32)
    cosine, sine_table = rope_angles(length + query_pos, head_size)
    queries = rotate_pairs(projected[:, 0], cosine, sine_table).astype(jnp.bfloat16)
    new_keys = rotate_pairs(projected[:, 1], cosine, sine_table).astype(jnp.bfloat16)
    new_values = projected[:, 2].astype(jnp.bfloat16)
    fresh_kv = jnp.stack(
        [
            new_keys.reshape(stretch_rows, local_width),
            new_values.reshape(stretch_rows, local_width),
        ],
        axis=0,
    )
    local_kv = jnp.concatenate([prompt_cache[0, 0], fresh_kv], axis=1)
    block_span = cache_rows + stretch_rows

    def attend_rows(carry, kv_piece, source):
        row_peak, totals, accumulated = carry
        piece_rows = kv_piece.shape[1]
        offset = jnp.arange(piece_rows, dtype=jnp.int32)
        from_cache = offset < cache_rows
        cache_pos = source * cache_rows + offset
        stretch_pos = source * stretch_rows + offset - cache_rows
        allowed = jnp.where(
            from_cache[None, :],
            cache_pos[None, :] < length,
            stretch_pos[None, :] <= query_pos[:, None],
        )
        piece_keys = kv_piece[0].reshape(piece_rows, local_heads, head_size)
        piece_values = kv_piece[1].reshape(piece_rows, local_heads, head_size)
        scores = (
            jnp.einsum("qhe,khe->hqk", queries, piece_keys, preferred_element_type=jnp.float32)
            * scale_factor
        )
        key_gate = allowed[None]
        masked = jnp.where(key_gate, scores, NEG_FLOOR)
        new_peak = jnp.maximum(row_peak, jnp.max(masked, axis=2))
        shrink = jnp.exp(row_peak - new_peak)
        weights = jnp.where(key_gate, jnp.exp(masked - new_peak[..., None]), 0.0)
        totals = totals * shrink + jnp.sum(weights, axis=2)
        update = jnp.einsum(
            "hqk,khe->qhe",
            weights.astype(jnp.bfloat16),
            piece_values,
            preferred_element_type=jnp.float32,
        )
        accumulated = accumulated * jnp.transpose(shrink)[:, :, None] + update
        return (new_peak, totals, accumulated)

    state = (
        jnp.full((local_heads, stretch_rows), NEG_FLOOR, jnp.float32),
        jnp.zeros((local_heads, stretch_rows), jnp.float32),
        jnp.zeros((stretch_rows, local_heads, head_size), jnp.float32),
    )
    kv_pieces = gather_shifts(local_kv, "req", n_req)
    state = attend_rows(state, kv_pieces[0], block_id)
    remote_kv = jnp.stack(kv_pieces[1:], axis=0)

    def remote_block(step, inner_state):
        piece = lax.dynamic_index_in_dim(remote_kv, step, 0, keepdims=False)
        return attend_rows(inner_state, piece, (block_id - step - 1) % n_req)

    state = lax.fori_loop(0, n_req - 1, remote_block, state)
    row_peak, totals, accumulated = state
    attended = (
        (accumulated / jnp.transpose(totals)[:, :, None])
        .astype(jnp.bfloat16)
        .reshape(stretch_rows, local_width)
    )
    out_weight_t = lax.all_gather(jnp.transpose(w_out), ("grp", "req"), axis=0, tiled=True)
    branch = None
    for shift in range(n_tp):
        target = (tensor_id + shift) % n_tp
        weight_block = lax.dynamic_slice_in_dim(out_weight_t, target * local_width, local_width, 0)
        product = lax.dot_general(
            attended,
            weight_block,
            (((1,), (1,)), ((), ())),
            preferred_element_type=jnp.float32,
        ).astype(jnp.bfloat16)
        if shift:
            product = lax.ppermute(
                product, "tp", [(i, (i + shift) % n_tp) for i in range(n_tp)]
            )
        term = product.astype(jnp.float32)
        branch = term if branch is None else branch + term
    branch = branch.astype(jnp.bfloat16)

    return (branch[None], result[None])


def solution(mesh):
    placed = (
        P("grp", "req", "tp"),
        P(),
        P(("grp", "req"), None, "tp"),
        P("tp", ("grp", "req")),
        P("grp", None, None, "req", "tp"),
        P(),
        P(),
        P(),
        P(),
        P(("grp", "req"), None, None, "tp"),
        P(("grp", "req"), None, None, None, "tp"),
    )
    return jax.shard_map(
        per_device,
        mesh=mesh,
        in_specs=placed,
        out_specs=(P("grp", "req", "tp"), P(("grp", "req"), None, None, "tp")),
        check_vma=False,
    )
```

```python
import jax
import jax.numpy as jnp
from jax import lax
from jax.sharding import PartitionSpec as P

HD = 96


NEG_FLOOR = -1e30
NORM_EPS = 1e-05
ROPE_BASE = 10000.0


def rope_angles(positions, head_size):
    half_size = head_size // 2
    freqs = ROPE_BASE ** (-(jnp.arange(half_size, dtype=jnp.float32) * 2.0 / head_size))
    angles = positions.astype(jnp.float32)[:, None] * freqs[None, :]
    return (jnp.cos(angles), jnp.sin(angles))


def rotate_pairs(values, cosine, sine_table):
    half_size = values.shape[-1] // 2
    first_half = values[..., :half_size]
    second_half = values[..., half_size:]
    cos_b = cosine[:, None, :]
    sin_b = sine_table[:, None, :]
    return jnp.concatenate(
        [first_half * cos_b - second_half * sin_b, second_half * cos_b + first_half * sin_b],
        axis=-1,
    )


def exact_round(values):
    return lax.optimization_barrier(values.astype(jnp.bfloat16)).astype(jnp.float32)


def cache_partial(queries, cache_keys, cache_values, allowed, scale_factor):
    scores = (
        jnp.einsum("slhe,lkhe->slhk", queries, cache_keys, preferred_element_type=jnp.float32)
        * scale_factor
    )
    key_gate = allowed[:, None, None, :]
    masked = jnp.where(key_gate, scores, NEG_FLOOR)
    row_peak = jnp.max(masked, axis=3)
    weights = jnp.where(key_gate, jnp.exp(masked - row_peak[..., None]), 0.0)
    totals = jnp.sum(weights, axis=3)
    accumulated = jnp.einsum(
        "slhk,lkhe->slhe",
        weights.astype(jnp.bfloat16),
        cache_values,
        preferred_element_type=jnp.float32,
    )
    return (row_peak, totals, accumulated)


def finish_slots(merged, own_query, own_kv, own_alive, scale_factor):
    row_peak, totals, accumulated = merged
    own_key = own_kv[:, :, 0]
    own_value = own_kv[:, :, 1]
    own_score = (
        jnp.einsum("slhe,slhe->slh", own_query, own_key, preferred_element_type=jnp.float32)
        * scale_factor
    )
    new_peak = jnp.maximum(row_peak, own_score)
    shrink = jnp.exp(row_peak - new_peak)
    own_weight = jnp.exp(own_score - new_peak)
    new_total = totals * shrink + own_weight
    mixed = accumulated * shrink[..., None] + exact_round(own_weight)[..., None] * own_value.astype(
        jnp.float32
    )
    result = mixed / new_total[..., None]
    result = jnp.where(own_alive[:, None, None, None], result, 0.0)
    return result.astype(jnp.bfloat16)


def gather_shifts(value, axis, count):
    pieces = [value]
    for shift in range(1, count):
        pieces.append(
            lax.ppermute(value, axis, [(i, (i + shift) % count) for i in range(count)])
        )
    return pieces


def decode_slots(
    block_id, group_id, replica_id, n_req, n_grp, local_heads, head_size, scale_factor,
    prompt_cache, req_count, req_map, prefix_len, slot_query, slot_new_kv,
):
    cache_rows = prompt_cache.shape[3]
    layer_count = prompt_cache.shape[1]
    slot_count = slot_query.shape[1]
    group_total, max_requests = req_map.shape
    flat_count = group_total * max_requests
    request_ids = jnp.arange(flat_count, dtype=jnp.int32)
    group_of = request_ids // max_requests
    count_of = jnp.sum(
        jnp.where(
            group_of[:, None] == jnp.arange(group_total, dtype=jnp.int32)[None, :],
            req_count[None, :],
            0,
        ),
        axis=1,
    )
    request_live = request_ids % max_requests < count_of
    flat_map = req_map.reshape(flat_count)
    earlier = (
        (flat_map[None, :] == flat_map[:, None])
        & request_live[None, :]
        & (request_ids[None, :] < request_ids[:, None])
    )
    order_rank = jnp.sum(earlier.astype(jnp.int32), axis=1)
    slot_of = jnp.where(request_live, flat_map * slot_count + order_rank, 0)
    prefix_flat = prefix_len.reshape(flat_count)
    first_request = group_id * max_requests
    mine_live = lax.dynamic_slice_in_dim(request_live, first_request, max_requests, 0)
    mine_slot = lax.dynamic_slice_in_dim(slot_of, first_request, max_requests, 0)
    mine_prefix = lax.dynamic_slice_in_dim(prefix_flat, first_request, max_requests, 0)
    by_block = jnp.concatenate(gather_shifts(slot_query[0], "req", n_req), axis=0)
    all_queries = jnp.concatenate(gather_shifts(by_block, "grp", n_grp), axis=0)
    home_replica = mine_slot // slot_count
    query_row = (
        ((group_id - home_replica // n_req) % n_grp) * (n_req * slot_count)
        + ((block_id - home_replica % n_req) % n_req) * slot_count
        + mine_slot % slot_count
    )
    picked = jnp.take(all_queries, query_row, axis=0).reshape(
        max_requests, layer_count, local_heads, head_size
    )
    cache_keys = prompt_cache[0, :, 0].reshape(layer_count, cache_rows, local_heads, head_size)
    cache_values = prompt_cache[0, :, 1].reshape(layer_count, cache_rows, local_heads, head_size)
    cache_pos = block_id * cache_rows + jnp.arange(cache_rows, dtype=jnp.int32)
    allowed = mine_live[:, None] & (cache_pos[None, :] < mine_prefix[:, None])
    part_peak, part_total, part_accum = cache_partial(
        picked, cache_keys, cache_values, allowed, scale_factor
    )
    packed = jnp.concatenate([part_peak[..., None], part_total[..., None], part_accum], axis=-1)
    block_parts = jnp.stack(gather_shifts(packed, "req", n_req), axis=0)
    peaks = block_parts[..., 0]
    group_peak = jnp.max(peaks, axis=0)
    factor = jnp.exp(peaks - group_peak[None])
    group_total_w = jnp.sum(block_parts[..., 1] * factor, axis=0)
    group_accum = jnp.sum(block_parts[..., 2:] * factor[..., None], axis=0)
    merged_group = jnp.concatenate(
        [group_peak[..., None], group_total_w[..., None], group_accum], axis=-1
    )
    every_group = jnp.concatenate(gather_shifts(merged_group, "grp", n_grp), axis=0)
    slot_hit = (
        request_live[None, :]
        & (flat_map[None, :] == replica_id)
        & (order_rank[None, :] == jnp.arange(slot_count, dtype=jnp.int32)[:, None])
    )
    own_request = jnp.sum(jnp.where(slot_hit, request_ids[None, :], 0), axis=1)
    own_alive = jnp.any(slot_hit, axis=1)
    home_shift = (group_id - own_request // max_requests) % n_grp
    own_state = jnp.take(
        every_group, home_shift * max_requests + own_request % max_requests, axis=0
    )
    merged = (own_state[..., 0], own_state[..., 1], own_state[..., 2:])
    own_query = slot_query[0].reshape(slot_count, layer_count, local_heads, head_size)
    own_kv = slot_new_kv[0].reshape(slot_count, layer_count, 2, local_heads, head_size)
    result = finish_slots(merged, own_query, own_kv, own_alive, scale_factor)
    return result.reshape(slot_count, layer_count, local_heads * head_size)


def per_device(
    stretch_in,
    norm_gain,
    w_qkv,
    w_out,
    prompt_cache,
    prompt_len,
    req_count,
    req_map,
    prefix_len,
    slot_query,
    slot_new_kv,
):
    group_id = lax.axis_index("grp")
    block_id = lax.axis_index("req")
    tensor_id = lax.axis_index("tp")
    replica_id = lax.axis_index(("grp", "req"))
    n_tp = lax.axis_size("tp")
    n_req = lax.axis_size("req")
    n_grp = lax.axis_size("grp")
    stretch_rows = stretch_in.shape[1]
    local_width = stretch_in.shape[2]
    tensor_width = local_width * n_tp
    head_size = HD
    local_heads = local_width // head_size
    cache_rows = prompt_cache.shape[3]
    layer_count = prompt_cache.shape[1]
    slot_count = slot_query.shape[1]
    scale_factor = head_size ** (-0.5)
    length = lax.dynamic_index_in_dim(prompt_len, group_id, 0, keepdims=False)

    rows_in = stretch_in[0]
    row_pieces = gather_shifts(rows_in, "tp", n_tp)
    full_rows = jnp.zeros((stretch_rows, tensor_width), rows_in.dtype)
    for shift, piece in enumerate(row_pieces):
        source = (tensor_id - shift) % n_tp
        full_rows = lax.dynamic_update_slice_in_dim(full_rows, piece, source * local_width, 1)
    widened = full_rows.astype(jnp.float32)
    mean_square = jnp.mean(widened * widened, axis=1, keepdims=True)
    normed = (widened * lax.rsqrt(mean_square + NORM_EPS) * norm_gain.astype(jnp.float32)).astype(
        jnp.bfloat16
    )

    qkv_cols = w_qkv.shape[1] * w_qkv.shape[2]
    both_weights = jnp.concatenate(
        [w_qkv.reshape(w_qkv.shape[0], qkv_cols), jnp.transpose(w_out)], axis=1
    )
    both_weights = lax.all_gather(both_weights, ("grp", "req"), axis=0, tiled=True)
    weight_piece = both_weights[:, :qkv_cols]
    out_weight_t = both_weights[:, qkv_cols:]
    result = decode_slots(
        block_id, group_id, replica_id, n_req, n_grp, local_heads, head_size, scale_factor,
        prompt_cache, req_count, req_map, prefix_len, slot_query, slot_new_kv,
    )
    normed, result = lax.optimization_barrier((normed, result))

    projected = jnp.dot(normed, weight_piece, preferred_element_type=jnp.float32)
    projected = projected.reshape(stretch_rows, 3, local_heads, head_size)
    query_pos = block_id * stretch_rows + jnp.arange(stretch_rows, dtype=jnp.int32)
    cosine, sine_table = rope_angles(length + query_pos, head_size)
    queries = rotate_pairs(projected[:, 0], cosine, sine_table).astype(jnp.bfloat16)
    new_keys = rotate_pairs(projected[:, 1], cosine, sine_table).astype(jnp.bfloat16)
    new_values = projected[:, 2].astype(jnp.bfloat16)
    fresh_kv = jnp.stack(
        [
            new_keys.reshape(stretch_rows, local_width),
            new_values.reshape(stretch_rows, local_width),
        ],
        axis=0,
    )
    local_kv = jnp.concatenate([prompt_cache[0, 0], fresh_kv], axis=1)
    block_span = cache_rows + stretch_rows

    def attend_rows(carry, kv_piece, source):
        row_peak, totals, accumulated = carry
        piece_rows = kv_piece.shape[1]
        offset = jnp.arange(piece_rows, dtype=jnp.int32)
        from_cache = offset < cache_rows
        cache_pos = source * cache_rows + offset
        stretch_pos = source * stretch_rows + offset - cache_rows
        allowed = jnp.where(
            from_cache[None, :],
            cache_pos[None, :] < length,
            stretch_pos[None, :] <= query_pos[:, None],
        )
        piece_keys = kv_piece[0].reshape(piece_rows, local_heads, head_size)
        piece_values = kv_piece[1].reshape(piece_rows, local_heads, head_size)
        scores = (
            jnp.einsum("qhe,khe->hqk", queries, piece_keys, preferred_element_type=jnp.float32)
            * scale_factor
        )
        key_gate = allowed[None]
        masked = jnp.where(key_gate, scores, NEG_FLOOR)
        new_peak = jnp.maximum(row_peak, jnp.max(masked, axis=2))
        shrink = jnp.exp(row_peak - new_peak)
        weights = jnp.where(key_gate, jnp.exp(masked - new_peak[..., None]), 0.0)
        totals = totals * shrink + jnp.sum(weights, axis=2)
        update = jnp.einsum(
            "hqk,khe->qhe",
            weights.astype(jnp.bfloat16),
            piece_values,
            preferred_element_type=jnp.float32,
        )
        accumulated = accumulated * jnp.transpose(shrink)[:, :, None] + update
        return (new_peak, totals, accumulated)

    state = (
        jnp.full((local_heads, stretch_rows), NEG_FLOOR, jnp.float32),
        jnp.zeros((local_heads, stretch_rows), jnp.float32),
        jnp.zeros((stretch_rows, local_heads, head_size), jnp.float32),
    )
    kv_pieces = gather_shifts(local_kv, "req", n_req)
    state = attend_rows(state, kv_pieces[0], block_id)
    remote_kv = jnp.stack(kv_pieces[1:], axis=0)

    def remote_block(step, inner_state):
        piece = lax.dynamic_index_in_dim(remote_kv, step, 0, keepdims=False)
        return attend_rows(inner_state, piece, (block_id - step - 1) % n_req)

    state = lax.fori_loop(0, n_req - 1, remote_block, state)
    row_peak, totals, accumulated = state
    attended = (
        (accumulated / jnp.transpose(totals)[:, :, None])
        .astype(jnp.bfloat16)
        .reshape(stretch_rows, local_width)
    )
    branch = None
    for shift in range(n_tp):
        target = (tensor_id + shift) % n_tp
        weight_block = lax.dynamic_slice_in_dim(out_weight_t, target * local_width, local_width, 0)
        product = lax.dot_general(
            attended,
            weight_block,
            (((1,), (1,)), ((), ())),
            preferred_element_type=jnp.float32,
        ).astype(jnp.bfloat16)
        if shift:
            product = lax.ppermute(
                product, "tp", [(i, (i + shift) % n_tp) for i in range(n_tp)]
            )
        term = product.astype(jnp.float32)
        branch = term if branch is None else branch + term
    branch = branch.astype(jnp.bfloat16)

    return (branch[None], result[None])


def solution(mesh):
    placed = (
        P("grp", "req", "tp"),
        P(),
        P(("grp", "req"), None, "tp"),
        P("tp", ("grp", "req")),
        P("grp", None, None, "req", "tp"),
        P(),
        P(),
        P(),
        P(),
        P(("grp", "req"), None, None, "tp"),
        P(("grp", "req"), None, None, None, "tp"),
    )
    return jax.shard_map(
        per_device,
        mesh=mesh,
        in_specs=placed,
        out_specs=(P("grp", "req", "tp"), P(("grp", "req"), None, None, "tp")),
        check_vma=False,
    )
```

```python
import jax
import jax.numpy as jnp
from jax import lax
from jax.sharding import PartitionSpec as P

HD = 96


NEG_FLOOR = -1e30
NORM_EPS = 1e-05
ROPE_BASE = 10000.0


def rope_angles(positions, head_size):
    half_size = head_size // 2
    freqs = ROPE_BASE ** (-(jnp.arange(half_size, dtype=jnp.float32) * 2.0 / head_size))
    angles = positions.astype(jnp.float32)[:, None] * freqs[None, :]
    return (jnp.cos(angles), jnp.sin(angles))


def rotate_pairs(values, cosine, sine_table):
    half_size = values.shape[-1] // 2
    first_half = values[..., :half_size]
    second_half = values[..., half_size:]
    cos_b = cosine[:, None, :]
    sin_b = sine_table[:, None, :]
    return jnp.concatenate(
        [first_half * cos_b - second_half * sin_b, second_half * cos_b + first_half * sin_b],
        axis=-1,
    )


def exact_round(values):
    return lax.optimization_barrier(values.astype(jnp.bfloat16)).astype(jnp.float32)


def cache_partial(queries, cache_keys, cache_values, allowed, scale_factor):
    scores = (
        jnp.einsum("slhe,lkhe->slhk", queries, cache_keys, preferred_element_type=jnp.float32)
        * scale_factor
    )
    key_gate = allowed[:, None, None, :]
    masked = jnp.where(key_gate, scores, NEG_FLOOR)
    row_peak = jnp.max(masked, axis=3)
    weights = jnp.where(key_gate, jnp.exp(masked - row_peak[..., None]), 0.0)
    totals = jnp.sum(weights, axis=3)
    accumulated = jnp.einsum(
        "slhk,lkhe->slhe",
        weights.astype(jnp.bfloat16),
        cache_values,
        preferred_element_type=jnp.float32,
    )
    return (row_peak, totals, accumulated)


def finish_slots(merged, own_query, own_kv, own_alive, scale_factor):
    row_peak, totals, accumulated = merged
    own_key = own_kv[:, :, 0]
    own_value = own_kv[:, :, 1]
    own_score = (
        jnp.einsum("slhe,slhe->slh", own_query, own_key, preferred_element_type=jnp.float32)
        * scale_factor
    )
    new_peak = jnp.maximum(row_peak, own_score)
    shrink = jnp.exp(row_peak - new_peak)
    own_weight = jnp.exp(own_score - new_peak)
    new_total = totals * shrink + own_weight
    mixed = accumulated * shrink[..., None] + exact_round(own_weight)[..., None] * own_value.astype(
        jnp.float32
    )
    result = mixed / new_total[..., None]
    result = jnp.where(own_alive[:, None, None, None], result, 0.0)
    return result.astype(jnp.bfloat16)


def gather_shifts(value, axis, count):
    pieces = [value]
    for shift in range(1, count):
        pieces.append(
            lax.ppermute(value, axis, [(i, (i + shift) % count) for i in range(count)])
        )
    return pieces


def decode_slots(
    block_id, group_id, replica_id, n_req, n_grp, local_heads, head_size, scale_factor,
    prompt_cache, req_count, req_map, prefix_len, slot_query, slot_new_kv,
):
    cache_rows = prompt_cache.shape[3]
    layer_count = prompt_cache.shape[1]
    slot_count = slot_query.shape[1]
    group_total, max_requests = req_map.shape
    flat_count = group_total * max_requests
    request_ids = jnp.arange(flat_count, dtype=jnp.int32)
    group_of = request_ids // max_requests
    count_of = jnp.sum(
        jnp.where(
            group_of[:, None] == jnp.arange(group_total, dtype=jnp.int32)[None, :],
            req_count[None, :],
            0,
        ),
        axis=1,
    )
    request_live = request_ids % max_requests < count_of
    flat_map = req_map.reshape(flat_count)
    earlier = (
        (flat_map[None, :] == flat_map[:, None])
        & request_live[None, :]
        & (request_ids[None, :] < request_ids[:, None])
    )
    order_rank = jnp.sum(earlier.astype(jnp.int32), axis=1)
    slot_of = jnp.where(request_live, flat_map * slot_count + order_rank, 0)
    prefix_flat = prefix_len.reshape(flat_count)
    first_request = group_id * max_requests
    mine_live = lax.dynamic_slice_in_dim(request_live, first_request, max_requests, 0)
    mine_slot = lax.dynamic_slice_in_dim(slot_of, first_request, max_requests, 0)
    mine_prefix = lax.dynamic_slice_in_dim(prefix_flat, first_request, max_requests, 0)
    by_block = jnp.concatenate(gather_shifts(slot_query[0], "req", n_req), axis=0)
    all_queries = jnp.concatenate(gather_shifts(by_block, "grp", n_grp), axis=0)
    home_replica = mine_slot // slot_count
    query_row = (
        ((group_id - home_replica // n_req) % n_grp) * (n_req * slot_count)
        + ((block_id - home_replica % n_req) % n_req) * slot_count
        + mine_slot % slot_count
    )
    picked = jnp.take(all_queries, query_row, axis=0).reshape(
        max_requests, layer_count, local_heads, head_size
    )
    cache_keys = prompt_cache[0, :, 0].reshape(layer_count, cache_rows, local_heads, head_size)
    cache_values = prompt_cache[0, :, 1].reshape(layer_count, cache_rows, local_heads, head_size)
    cache_pos = block_id * cache_rows + jnp.arange(cache_rows, dtype=jnp.int32)
    allowed = mine_live[:, None] & (cache_pos[None, :] < mine_prefix[:, None])
    part_peak, part_total, part_accum = cache_partial(
        picked, cache_keys, cache_values, allowed, scale_factor
    )
    packed = jnp.concatenate([part_peak[..., None], part_total[..., None], part_accum], axis=-1)
    block_parts = jnp.stack(gather_shifts(packed, "req", n_req), axis=0)
    peaks = block_parts[..., 0]
    group_peak = jnp.max(peaks, axis=0)
    factor = jnp.exp(peaks - group_peak[None])
    group_total_w = jnp.sum(block_parts[..., 1] * factor, axis=0)
    group_accum = jnp.sum(block_parts[..., 2:] * factor[..., None], axis=0)
    merged_group = jnp.concatenate(
        [group_peak[..., None], group_total_w[..., None], group_accum], axis=-1
    )
    every_group = jnp.concatenate(gather_shifts(merged_group, "grp", n_grp), axis=0)
    slot_hit = (
        request_live[None, :]
        & (flat_map[None, :] == replica_id)
        & (order_rank[None, :] == jnp.arange(slot_count, dtype=jnp.int32)[:, None])
    )
    own_request = jnp.sum(jnp.where(slot_hit, request_ids[None, :], 0), axis=1)
    own_alive = jnp.any(slot_hit, axis=1)
    home_shift = (group_id - own_request // max_requests) % n_grp
    own_state = jnp.take(
        every_group, home_shift * max_requests + own_request % max_requests, axis=0
    )
    merged = (own_state[..., 0], own_state[..., 1], own_state[..., 2:])
    own_query = slot_query[0].reshape(slot_count, layer_count, local_heads, head_size)
    own_kv = slot_new_kv[0].reshape(slot_count, layer_count, 2, local_heads, head_size)
    result = finish_slots(merged, own_query, own_kv, own_alive, scale_factor)
    return result.reshape(slot_count, layer_count, local_heads * head_size)


def per_device(
    stretch_in,
    norm_gain,
    w_qkv,
    w_out,
    prompt_cache,
    prompt_len,
    req_count,
    req_map,
    prefix_len,
    slot_query,
    slot_new_kv,
):
    group_id = lax.axis_index("grp")
    block_id = lax.axis_index("req")
    tensor_id = lax.axis_index("tp")
    replica_id = lax.axis_index(("grp", "req"))
    n_tp = lax.axis_size("tp")
    n_req = lax.axis_size("req")
    n_grp = lax.axis_size("grp")
    stretch_rows = stretch_in.shape[1]
    local_width = stretch_in.shape[2]
    tensor_width = local_width * n_tp
    head_size = HD
    local_heads = local_width // head_size
    cache_rows = prompt_cache.shape[3]
    layer_count = prompt_cache.shape[1]
    slot_count = slot_query.shape[1]
    scale_factor = head_size ** (-0.5)
    length = lax.dynamic_index_in_dim(prompt_len, group_id, 0, keepdims=False)

    rows_in = stretch_in[0]
    x_half = tensor_id % 2
    y_index = tensor_id // 2
    y_count = n_tp // 2
    x_swap = [(i, i ^ 1) for i in range(n_tp)]
    neighbour_rows = lax.ppermute(rows_in, "tp", x_swap)
    row_pair = jnp.where(
        x_half == 0,
        jnp.concatenate([rows_in, neighbour_rows], axis=1),
        jnp.concatenate([neighbour_rows, rows_in], axis=1),
    )
    full_rows = jnp.zeros((stretch_rows, tensor_width), rows_in.dtype)
    full_rows = lax.dynamic_update_slice_in_dim(full_rows, row_pair, y_index * 2 * local_width, 1)
    for shift in range(1, y_count):
        moved = lax.ppermute(
            row_pair,
            "tp",
            [(i, (i + 2 * shift) % n_tp) for i in range(n_tp)],
        )
        source = (y_index - shift) % y_count
        full_rows = lax.dynamic_update_slice_in_dim(full_rows, moved, source * 2 * local_width, 1)
    widened = full_rows.astype(jnp.float32)
    mean_square = jnp.mean(widened * widened, axis=1, keepdims=True)
    normed = (widened * lax.rsqrt(mean_square + NORM_EPS) * norm_gain.astype(jnp.float32)).astype(
        jnp.bfloat16
    )

    qkv_cols = w_qkv.shape[1] * w_qkv.shape[2]
    both_weights = jnp.concatenate(
        [w_qkv.reshape(w_qkv.shape[0], qkv_cols), jnp.transpose(w_out)], axis=1
    )
    both_weights = lax.all_gather(both_weights, ("grp", "req"), axis=0, tiled=True)
    weight_piece = both_weights[:, :qkv_cols]
    out_weight_t = both_weights[:, qkv_cols:]
    result = decode_slots(
        block_id, group_id, replica_id, n_req, n_grp, local_heads, head_size, scale_factor,
        prompt_cache, req_count, req_map, prefix_len, slot_query, slot_new_kv,
    )
    normed, result = lax.optimization_barrier((normed, result))

    projected = jnp.dot(normed, weight_piece, preferred_element_type=jnp.float32)
    projected = projected.reshape(stretch_rows, 3, local_heads, head_size)
    query_pos = block_id * stretch_rows + jnp.arange(stretch_rows, dtype=jnp.int32)
    cosine, sine_table = rope_angles(length + query_pos, head_size)
    queries = rotate_pairs(projected[:, 0], cosine, sine_table).astype(jnp.bfloat16)
    new_keys = rotate_pairs(projected[:, 1], cosine, sine_table).astype(jnp.bfloat16)
    new_values = projected[:, 2].astype(jnp.bfloat16)
    fresh_kv = jnp.stack(
        [
            new_keys.reshape(stretch_rows, local_width),
            new_values.reshape(stretch_rows, local_width),
        ],
        axis=0,
    )
    local_kv = jnp.concatenate([prompt_cache[0, 0], fresh_kv], axis=1)
    block_span = cache_rows + stretch_rows

    def attend_rows(carry, kv_piece, source):
        row_peak, totals, accumulated = carry
        piece_rows = kv_piece.shape[1]
        offset = jnp.arange(piece_rows, dtype=jnp.int32)
        from_cache = offset < cache_rows
        cache_pos = source * cache_rows + offset
        stretch_pos = source * stretch_rows + offset - cache_rows
        allowed = jnp.where(
            from_cache[None, :],
            cache_pos[None, :] < length,
            stretch_pos[None, :] <= query_pos[:, None],
        )
        piece_keys = kv_piece[0].reshape(piece_rows, local_heads, head_size)
        piece_values = kv_piece[1].reshape(piece_rows, local_heads, head_size)
        scores = (
            jnp.einsum("qhe,khe->hqk", queries, piece_keys, preferred_element_type=jnp.float32)
            * scale_factor
        )
        key_gate = allowed[None]
        masked = jnp.where(key_gate, scores, NEG_FLOOR)
        new_peak = jnp.maximum(row_peak, jnp.max(masked, axis=2))
        shrink = jnp.exp(row_peak - new_peak)
        weights = jnp.where(key_gate, jnp.exp(masked - new_peak[..., None]), 0.0)
        totals = totals * shrink + jnp.sum(weights, axis=2)
        update = jnp.einsum(
            "hqk,khe->qhe",
            weights.astype(jnp.bfloat16),
            piece_values,
            preferred_element_type=jnp.float32,
        )
        accumulated = accumulated * jnp.transpose(shrink)[:, :, None] + update
        return (new_peak, totals, accumulated)

    state = (
        jnp.full((local_heads, stretch_rows), NEG_FLOOR, jnp.float32),
        jnp.zeros((local_heads, stretch_rows), jnp.float32),
        jnp.zeros((stretch_rows, local_heads, head_size), jnp.float32),
    )
    chip_swap = [(i, i ^ 2) for i in range(n_req)]
    partner_cache = lax.ppermute(prompt_cache[0, 0], "req", chip_swap)
    partner_fresh = lax.ppermute(
        fresh_kv, "req", [(i, i ^ 2) for i in range(n_req) if i < (i ^ 2)]
    )
    partner_kv = jnp.concatenate([partner_cache, partner_fresh], axis=1)
    core_pair = jnp.stack([local_kv, partner_kv], axis=0)
    sibling_kv = lax.ppermute(core_pair, "req", [(i, i ^ 1) for i in range(n_req)])
    state = attend_rows(state, local_kv, block_id)
    remote_kv = jnp.concatenate([partner_kv[None], sibling_kv], axis=0)
    remote_xor = jnp.array([2, 1, 3], dtype=jnp.int32)

    def remote_block(step, inner_state):
        piece = lax.dynamic_index_in_dim(remote_kv, step, 0, keepdims=False)
        return attend_rows(inner_state, piece, jnp.bitwise_xor(block_id, remote_xor[step]))

    state = lax.fori_loop(0, n_req - 1, remote_block, state)
    row_peak, totals, accumulated = state
    attended = (
        (accumulated / jnp.transpose(totals)[:, :, None])
        .astype(jnp.bfloat16)
        .reshape(stretch_rows, local_width)
    )
    products = []
    for target in range(n_tp):
        weight_block = out_weight_t[target * local_width : (target + 1) * local_width]
        products.append(
            lax.dot_general(
                attended,
                weight_block,
                (((1,), (1,)), ((), ())),
                preferred_element_type=jnp.float32,
            ).astype(jnp.bfloat16)
        )
    by_target = jnp.stack(products, axis=0).reshape(y_count, 2, stretch_rows, local_width)
    kept = lax.dynamic_index_in_dim(by_target, x_half, 1, keepdims=False)
    handed = lax.dynamic_index_in_dim(by_target, 1 - x_half, 1, keepdims=False)
    arrived = lax.ppermute(handed, "tp", x_swap)
    row_sums = kept.astype(jnp.float32) + arrived.astype(jnp.float32)
    branch = lax.dynamic_index_in_dim(row_sums, y_index, 0, keepdims=False)
    for shift in range(1, y_count):
        outgoing = lax.dynamic_index_in_dim(row_sums, (y_index + shift) % y_count, 0, keepdims=False)
        branch = branch + lax.ppermute(
            outgoing,
            "tp",
            [(i, (i + 2 * shift) % n_tp) for i in range(n_tp)],
        )
    branch = branch.astype(jnp.bfloat16)

    return (branch[None], result[None])


def solution(mesh):
    placed = (
        P("grp", "req", "tp"),
        P(),
        P(("grp", "req"), None, "tp"),
        P("tp", ("grp", "req")),
        P("grp", None, None, "req", "tp"),
        P(),
        P(),
        P(),
        P(),
        P(("grp", "req"), None, None, "tp"),
        P(("grp", "req"), None, None, None, "tp"),
    )
    return jax.shard_map(
        per_device,
        mesh=mesh,
        in_specs=placed,
        out_specs=(P("grp", "req", "tp"), P(("grp", "req"), None, None, "tp")),
        check_vma=False,
    )
```

```python
import jax
import jax.numpy as jnp
from jax import lax
from jax.sharding import PartitionSpec as P

HD = 96


NEG_FLOOR = -1e30
NORM_EPS = 1e-05
ROPE_BASE = 10000.0


def rope_angles(positions, head_size):
    half_size = head_size // 2
    freqs = ROPE_BASE ** (-(jnp.arange(half_size, dtype=jnp.float32) * 2.0 / head_size))
    angles = positions.astype(jnp.float32)[:, None] * freqs[None, :]
    return (jnp.cos(angles), jnp.sin(angles))


def rotate_pairs(values, cosine, sine_table):
    half_size = values.shape[-1] // 2
    first_half = values[..., :half_size]
    second_half = values[..., half_size:]
    cos_b = cosine[:, None, :]
    sin_b = sine_table[:, None, :]
    return jnp.concatenate(
        [first_half * cos_b - second_half * sin_b, second_half * cos_b + first_half * sin_b],
        axis=-1,
    )


def exact_round(values):
    return lax.optimization_barrier(values.astype(jnp.bfloat16)).astype(jnp.float32)


def cache_partial(queries, cache_keys, cache_values, allowed, scale_factor):
    scores = (
        jnp.einsum("slhe,lkhe->slhk", queries, cache_keys, preferred_element_type=jnp.float32)
        * scale_factor
    )
    key_gate = allowed[:, None, None, :]
    masked = jnp.where(key_gate, scores, NEG_FLOOR)
    row_peak = jnp.max(masked, axis=3)
    weights = jnp.where(key_gate, jnp.exp(masked - row_peak[..., None]), 0.0)
    totals = jnp.sum(weights, axis=3)
    accumulated = jnp.einsum(
        "slhk,lkhe->slhe",
        weights.astype(jnp.bfloat16),
        cache_values,
        preferred_element_type=jnp.float32,
    )
    return (row_peak, totals, accumulated)


def finish_slots(merged, own_query, own_kv, own_alive, scale_factor):
    row_peak, totals, accumulated = merged
    own_key = own_kv[:, :, 0]
    own_value = own_kv[:, :, 1]
    own_score = (
        jnp.einsum("slhe,slhe->slh", own_query, own_key, preferred_element_type=jnp.float32)
        * scale_factor
    )
    new_peak = jnp.maximum(row_peak, own_score)
    shrink = jnp.exp(row_peak - new_peak)
    own_weight = jnp.exp(own_score - new_peak)
    new_total = totals * shrink + own_weight
    mixed = accumulated * shrink[..., None] + exact_round(own_weight)[..., None] * own_value.astype(
        jnp.float32
    )
    result = mixed / new_total[..., None]
    result = jnp.where(own_alive[:, None, None, None], result, 0.0)
    return result.astype(jnp.bfloat16)


def gather_shifts(value, axis, count):
    pieces = [value]
    for shift in range(1, count):
        pieces.append(
            lax.ppermute(value, axis, [(i, (i + shift) % count) for i in range(count)])
        )
    return pieces


def decode_slots(
    block_id, group_id, replica_id, n_req, n_grp, local_heads, head_size, scale_factor,
    prompt_cache, req_count, req_map, prefix_len, slot_query, slot_new_kv,
):
    cache_rows = prompt_cache.shape[3]
    layer_count = prompt_cache.shape[1]
    slot_count = slot_query.shape[1]
    group_total, max_requests = req_map.shape
    flat_count = group_total * max_requests
    request_ids = jnp.arange(flat_count, dtype=jnp.int32)
    group_of = request_ids // max_requests
    count_of = jnp.sum(
        jnp.where(
            group_of[:, None] == jnp.arange(group_total, dtype=jnp.int32)[None, :],
            req_count[None, :],
            0,
        ),
        axis=1,
    )
    request_live = request_ids % max_requests < count_of
    flat_map = req_map.reshape(flat_count)
    earlier = (
        (flat_map[None, :] == flat_map[:, None])
        & request_live[None, :]
        & (request_ids[None, :] < request_ids[:, None])
    )
    order_rank = jnp.sum(earlier.astype(jnp.int32), axis=1)
    slot_of = jnp.where(request_live, flat_map * slot_count + order_rank, 0)
    prefix_flat = prefix_len.reshape(flat_count)
    first_request = group_id * max_requests
    mine_live = lax.dynamic_slice_in_dim(request_live, first_request, max_requests, 0)
    mine_slot = lax.dynamic_slice_in_dim(slot_of, first_request, max_requests, 0)
    mine_prefix = lax.dynamic_slice_in_dim(prefix_flat, first_request, max_requests, 0)
    by_block = jnp.concatenate(gather_shifts(slot_query[0], "req", n_req), axis=0)
    all_queries = jnp.concatenate(gather_shifts(by_block, "grp", n_grp), axis=0)
    home_replica = mine_slot // slot_count
    query_row = (
        ((group_id - home_replica // n_req) % n_grp) * (n_req * slot_count)
        + ((block_id - home_replica % n_req) % n_req) * slot_count
        + mine_slot % slot_count
    )
    picked = jnp.take(all_queries, query_row, axis=0).reshape(
        max_requests, layer_count, local_heads, head_size
    )
    cache_keys = prompt_cache[0, :, 0].reshape(layer_count, cache_rows, local_heads, head_size)
    cache_values = prompt_cache[0, :, 1].reshape(layer_count, cache_rows, local_heads, head_size)
    cache_pos = block_id * cache_rows + jnp.arange(cache_rows, dtype=jnp.int32)
    allowed = mine_live[:, None] & (cache_pos[None, :] < mine_prefix[:, None])
    part_peak, part_total, part_accum = cache_partial(
        picked, cache_keys, cache_values, allowed, scale_factor
    )
    packed = jnp.concatenate([part_peak[..., None], part_total[..., None], part_accum], axis=-1)
    block_parts = jnp.stack(gather_shifts(packed, "req", n_req), axis=0)
    peaks = block_parts[..., 0]
    group_peak = jnp.max(peaks, axis=0)
    factor = jnp.exp(peaks - group_peak[None])
    group_total_w = jnp.sum(block_parts[..., 1] * factor, axis=0)
    group_accum = jnp.sum(block_parts[..., 2:] * factor[..., None], axis=0)
    merged_group = jnp.concatenate(
        [group_peak[..., None], group_total_w[..., None], group_accum], axis=-1
    )
    every_group = jnp.concatenate(gather_shifts(merged_group, "grp", n_grp), axis=0)
    slot_hit = (
        request_live[None, :]
        & (flat_map[None, :] == replica_id)
        & (order_rank[None, :] == jnp.arange(slot_count, dtype=jnp.int32)[:, None])
    )
    own_request = jnp.sum(jnp.where(slot_hit, request_ids[None, :], 0), axis=1)
    own_alive = jnp.any(slot_hit, axis=1)
    home_shift = (group_id - own_request // max_requests) % n_grp
    own_state = jnp.take(
        every_group, home_shift * max_requests + own_request % max_requests, axis=0
    )
    merged = (own_state[..., 0], own_state[..., 1], own_state[..., 2:])
    own_query = slot_query[0].reshape(slot_count, layer_count, local_heads, head_size)
    own_kv = slot_new_kv[0].reshape(slot_count, layer_count, 2, local_heads, head_size)
    result = finish_slots(merged, own_query, own_kv, own_alive, scale_factor)
    return result.reshape(slot_count, layer_count, local_heads * head_size)


def per_device(
    stretch_in,
    norm_gain,
    w_qkv,
    w_out,
    prompt_cache,
    prompt_len,
    req_count,
    req_map,
    prefix_len,
    slot_query,
    slot_new_kv,
):
    group_id = lax.axis_index("grp")
    block_id = lax.axis_index("req")
    tensor_id = lax.axis_index("tp")
    replica_id = lax.axis_index(("grp", "req"))
    n_tp = lax.axis_size("tp")
    n_req = lax.axis_size("req")
    n_grp = lax.axis_size("grp")
    stretch_rows = stretch_in.shape[1]
    local_width = stretch_in.shape[2]
    tensor_width = local_width * n_tp
    head_size = HD
    local_heads = local_width // head_size
    cache_rows = prompt_cache.shape[3]
    layer_count = prompt_cache.shape[1]
    slot_count = slot_query.shape[1]
    scale_factor = head_size ** (-0.5)
    length = lax.dynamic_index_in_dim(prompt_len, group_id, 0, keepdims=False)

    rows_in = stretch_in[0]
    row_pieces = gather_shifts(rows_in, "tp", n_tp)
    full_rows = jnp.zeros((stretch_rows, tensor_width), rows_in.dtype)
    for shift, piece in enumerate(row_pieces):
        source = (tensor_id - shift) % n_tp
        full_rows = lax.dynamic_update_slice_in_dim(full_rows, piece, source * local_width, 1)
    widened = full_rows.astype(jnp.float32)
    mean_square = jnp.mean(widened * widened, axis=1, keepdims=True)
    normed = (widened * lax.rsqrt(mean_square + NORM_EPS) * norm_gain.astype(jnp.float32)).astype(
        jnp.bfloat16
    )

    qkv_cols = w_qkv.shape[1] * w_qkv.shape[2]
    both_weights = jnp.concatenate(
        [w_qkv.reshape(w_qkv.shape[0], qkv_cols), jnp.transpose(w_out)], axis=1
    )
    both_weights = lax.all_gather(both_weights, ("grp", "req"), axis=0, tiled=True)
    weight_piece = both_weights[:, :qkv_cols]
    out_weight_t = both_weights[:, qkv_cols:]
    result = decode_slots(
        block_id, group_id, replica_id, n_req, n_grp, local_heads, head_size, scale_factor,
        prompt_cache, req_count, req_map, prefix_len, slot_query, slot_new_kv,
    )
    normed, result = lax.optimization_barrier((normed, result))

    projected = jnp.dot(normed, weight_piece, preferred_element_type=jnp.float32)
    projected = projected.reshape(stretch_rows, 3, local_heads, head_size)
    query_pos = block_id * stretch_rows + jnp.arange(stretch_rows, dtype=jnp.int32)
    cosine, sine_table = rope_angles(length + query_pos, head_size)
    queries = rotate_pairs(projected[:, 0], cosine, sine_table).astype(jnp.bfloat16)
    new_keys = rotate_pairs(projected[:, 1], cosine, sine_table).astype(jnp.bfloat16)
    new_values = projected[:, 2].astype(jnp.bfloat16)
    fresh_kv = jnp.stack(
        [
            new_keys.reshape(stretch_rows, local_width),
            new_values.reshape(stretch_rows, local_width),
        ],
        axis=0,
    )
    local_kv = jnp.concatenate([prompt_cache[0, 0], fresh_kv], axis=1)
    block_span = cache_rows + stretch_rows

    def attend_rows(carry, kv_piece, source):
        row_peak, totals, accumulated = carry
        piece_rows = kv_piece.shape[1]
        offset = jnp.arange(piece_rows, dtype=jnp.int32)
        from_cache = offset < cache_rows
        cache_pos = source * cache_rows + offset
        stretch_pos = source * stretch_rows + offset - cache_rows
        allowed = jnp.where(
            from_cache[None, :],
            cache_pos[None, :] < length,
            stretch_pos[None, :] <= query_pos[:, None],
        )
        piece_keys = kv_piece[0].reshape(piece_rows, local_heads, head_size)
        piece_values = kv_piece[1].reshape(piece_rows, local_heads, head_size)
        scores = (
            jnp.einsum("qhe,khe->hqk", queries, piece_keys, preferred_element_type=jnp.float32)
            * scale_factor
        )
        key_gate = allowed[None]
        masked = jnp.where(key_gate, scores, NEG_FLOOR)
        new_peak = jnp.maximum(row_peak, jnp.max(masked, axis=2))
        shrink = jnp.exp(row_peak - new_peak)
        weights = jnp.where(key_gate, jnp.exp(masked - new_peak[..., None]), 0.0)
        totals = totals * shrink + jnp.sum(weights, axis=2)
        update = jnp.einsum(
            "hqk,khe->qhe",
            weights.astype(jnp.bfloat16),
            piece_values,
            preferred_element_type=jnp.float32,
        )
        accumulated = accumulated * jnp.transpose(shrink)[:, :, None] + update
        return (new_peak, totals, accumulated)

    state = (
        jnp.full((local_heads, stretch_rows), NEG_FLOOR, jnp.float32),
        jnp.zeros((local_heads, stretch_rows), jnp.float32),
        jnp.zeros((stretch_rows, local_heads, head_size), jnp.float32),
    )
    chip_swap = [(i, i ^ 2) for i in range(n_req)]
    upward = [(i, i ^ 2) for i in range(n_req) if i < (i ^ 2)]
    half_rows = stretch_rows // 2
    partner_cache = lax.ppermute(prompt_cache[0, 0], "req", chip_swap)
    partner_low = lax.ppermute(fresh_kv[:, :half_rows], "req", upward)
    partner_high = lax.ppermute(fresh_kv[:, half_rows:], "req", upward)
    partner_kv = jnp.concatenate([partner_cache, partner_low, partner_high], axis=1)
    core_pair = jnp.stack([local_kv, partner_kv], axis=0)
    sibling_kv = lax.ppermute(core_pair, "req", [(i, i ^ 1) for i in range(n_req)])
    state = attend_rows(state, local_kv, block_id)
    remote_kv = jnp.concatenate([partner_kv[None], sibling_kv], axis=0)
    remote_xor = jnp.array([2, 1, 3], dtype=jnp.int32)

    def remote_block(step, inner_state):
        piece = lax.dynamic_index_in_dim(remote_kv, step, 0, keepdims=False)
        return attend_rows(inner_state, piece, jnp.bitwise_xor(block_id, remote_xor[step]))

    state = lax.fori_loop(0, n_req - 1, remote_block, state)
    row_peak, totals, accumulated = state
    attended = (
        (accumulated / jnp.transpose(totals)[:, :, None])
        .astype(jnp.bfloat16)
        .reshape(stretch_rows, local_width)
    )
    branch = None
    for shift in range(n_tp):
        target = (tensor_id + shift) % n_tp
        weight_block = lax.dynamic_slice_in_dim(out_weight_t, target * local_width, local_width, 0)
        product = lax.dot_general(
            attended,
            weight_block,
            (((1,), (1,)), ((), ())),
            preferred_element_type=jnp.float32,
        ).astype(jnp.bfloat16)
        if shift:
            product = lax.ppermute(
                product, "tp", [(i, (i + shift) % n_tp) for i in range(n_tp)]
            )
        term = product.astype(jnp.float32)
        branch = term if branch is None else branch + term
    branch = branch.astype(jnp.bfloat16)

    return (branch[None], result[None])


def solution(mesh):
    placed = (
        P("grp", "req", "tp"),
        P(),
        P(("grp", "req"), None, "tp"),
        P("tp", ("grp", "req")),
        P("grp", None, None, "req", "tp"),
        P(),
        P(),
        P(),
        P(),
        P(("grp", "req"), None, None, "tp"),
        P(("grp", "req"), None, None, None, "tp"),
    )
    return jax.shard_map(
        per_device,
        mesh=mesh,
        in_specs=placed,
        out_specs=(P("grp", "req", "tp"), P(("grp", "req"), None, None, "tp")),
        check_vma=False,
    )
```

```python
import jax
import jax.numpy as jnp
from jax import lax
from jax.sharding import PartitionSpec as P

HD = 96


NEG_FLOOR = -1e30
NORM_EPS = 1e-05
ROPE_BASE = 10000.0


def rope_angles(positions, head_size):
    half_size = head_size // 2
    freqs = ROPE_BASE ** (-(jnp.arange(half_size, dtype=jnp.float32) * 2.0 / head_size))
    angles = positions.astype(jnp.float32)[:, None] * freqs[None, :]
    return (jnp.cos(angles), jnp.sin(angles))


def rotate_pairs(values, cosine, sine_table):
    half_size = values.shape[-1] // 2
    first_half = values[..., :half_size]
    second_half = values[..., half_size:]
    cos_b = cosine[:, None, :]
    sin_b = sine_table[:, None, :]
    return jnp.concatenate(
        [first_half * cos_b - second_half * sin_b, second_half * cos_b + first_half * sin_b],
        axis=-1,
    )


def exact_round(values):
    return lax.optimization_barrier(values.astype(jnp.bfloat16)).astype(jnp.float32)


def cache_partial(queries, cache_keys, cache_values, allowed, scale_factor):
    scores = (
        jnp.einsum("slhe,lkhe->slhk", queries, cache_keys, preferred_element_type=jnp.float32)
        * scale_factor
    )
    key_gate = allowed[:, None, None, :]
    masked = jnp.where(key_gate, scores, NEG_FLOOR)
    row_peak = jnp.max(masked, axis=3)
    weights = jnp.where(key_gate, jnp.exp(masked - row_peak[..., None]), 0.0)
    totals = jnp.sum(weights, axis=3)
    accumulated = jnp.einsum(
        "slhk,lkhe->slhe",
        weights.astype(jnp.bfloat16),
        cache_values,
        preferred_element_type=jnp.float32,
    )
    return (row_peak, totals, accumulated)


def finish_slots(merged, own_query, own_kv, own_alive, scale_factor):
    row_peak, totals, accumulated = merged
    own_key = own_kv[:, :, 0]
    own_value = own_kv[:, :, 1]
    own_score = (
        jnp.einsum("slhe,slhe->slh", own_query, own_key, preferred_element_type=jnp.float32)
        * scale_factor
    )
    new_peak = jnp.maximum(row_peak, own_score)
    shrink = jnp.exp(row_peak - new_peak)
    own_weight = jnp.exp(own_score - new_peak)
    new_total = totals * shrink + own_weight
    mixed = accumulated * shrink[..., None] + exact_round(own_weight)[..., None] * own_value.astype(
        jnp.float32
    )
    result = mixed / new_total[..., None]
    result = jnp.where(own_alive[:, None, None, None], result, 0.0)
    return result.astype(jnp.bfloat16)


def gather_shifts(value, axis, count):
    pieces = [value]
    for shift in range(1, count):
        pieces.append(
            lax.ppermute(value, axis, [(i, (i + shift) % count) for i in range(count)])
        )
    return pieces


def decode_slots(
    block_id, group_id, replica_id, n_req, n_grp, local_heads, head_size, scale_factor,
    prompt_cache, req_count, req_map, prefix_len, slot_query, slot_new_kv,
):
    cache_rows = prompt_cache.shape[3]
    layer_count = prompt_cache.shape[1]
    slot_count = slot_query.shape[1]
    group_total, max_requests = req_map.shape
    flat_count = group_total * max_requests
    request_ids = jnp.arange(flat_count, dtype=jnp.int32)
    group_of = request_ids // max_requests
    count_of = jnp.sum(
        jnp.where(
            group_of[:, None] == jnp.arange(group_total, dtype=jnp.int32)[None, :],
            req_count[None, :],
            0,
        ),
        axis=1,
    )
    request_live = request_ids % max_requests < count_of
    flat_map = req_map.reshape(flat_count)
    earlier = (
        (flat_map[None, :] == flat_map[:, None])
        & request_live[None, :]
        & (request_ids[None, :] < request_ids[:, None])
    )
    order_rank = jnp.sum(earlier.astype(jnp.int32), axis=1)
    slot_of = jnp.where(request_live, flat_map * slot_count + order_rank, 0)
    prefix_flat = prefix_len.reshape(flat_count)
    first_request = group_id * max_requests
    mine_live = lax.dynamic_slice_in_dim(request_live, first_request, max_requests, 0)
    mine_slot = lax.dynamic_slice_in_dim(slot_of, first_request, max_requests, 0)
    mine_prefix = lax.dynamic_slice_in_dim(prefix_flat, first_request, max_requests, 0)
    by_block = jnp.concatenate(gather_shifts(slot_query[0], "req", n_req), axis=0)
    all_queries = jnp.concatenate(gather_shifts(by_block, "grp", n_grp), axis=0)
    home_replica = mine_slot // slot_count
    query_row = (
        ((group_id - home_replica // n_req) % n_grp) * (n_req * slot_count)
        + ((block_id - home_replica % n_req) % n_req) * slot_count
        + mine_slot % slot_count
    )
    picked = jnp.take(all_queries, query_row, axis=0).reshape(
        max_requests, layer_count, local_heads, head_size
    )
    cache_keys = prompt_cache[0, :, 0].reshape(layer_count, cache_rows, local_heads, head_size)
    cache_values = prompt_cache[0, :, 1].reshape(layer_count, cache_rows, local_heads, head_size)
    cache_pos = block_id * cache_rows + jnp.arange(cache_rows, dtype=jnp.int32)
    allowed = mine_live[:, None] & (cache_pos[None, :] < mine_prefix[:, None])
    part_peak, part_total, part_accum = cache_partial(
        picked, cache_keys, cache_values, allowed, scale_factor
    )
    packed = jnp.concatenate([part_peak[..., None], part_total[..., None], part_accum], axis=-1)
    block_parts = jnp.stack(gather_shifts(packed, "req", n_req), axis=0)
    peaks = block_parts[..., 0]
    group_peak = jnp.max(peaks, axis=0)
    factor = jnp.exp(peaks - group_peak[None])
    group_total_w = jnp.sum(block_parts[..., 1] * factor, axis=0)
    group_accum = jnp.sum(block_parts[..., 2:] * factor[..., None], axis=0)
    merged_group = jnp.concatenate(
        [group_peak[..., None], group_total_w[..., None], group_accum], axis=-1
    )
    return merged_group


def finish_decode(
    merged_group, group_id, replica_id, n_grp, local_heads, head_size, scale_factor,
    prompt_cache, req_count, req_map, slot_query, slot_new_kv,
):
    layer_count = prompt_cache.shape[1]
    slot_count = slot_query.shape[1]
    group_total, max_requests = req_map.shape
    flat_count = group_total * max_requests
    request_ids = jnp.arange(flat_count, dtype=jnp.int32)
    group_of = request_ids // max_requests
    count_of = jnp.sum(
        jnp.where(
            group_of[:, None] == jnp.arange(group_total, dtype=jnp.int32)[None, :],
            req_count[None, :],
            0,
        ),
        axis=1,
    )
    request_live = request_ids % max_requests < count_of
    flat_map = req_map.reshape(flat_count)
    earlier = (
        (flat_map[None, :] == flat_map[:, None])
        & request_live[None, :]
        & (request_ids[None, :] < request_ids[:, None])
    )
    order_rank = jnp.sum(earlier.astype(jnp.int32), axis=1)
    every_group = jnp.concatenate(gather_shifts(merged_group, "grp", n_grp), axis=0)
    slot_hit = (
        request_live[None, :]
        & (flat_map[None, :] == replica_id)
        & (order_rank[None, :] == jnp.arange(slot_count, dtype=jnp.int32)[:, None])
    )
    own_request = jnp.sum(jnp.where(slot_hit, request_ids[None, :], 0), axis=1)
    own_alive = jnp.any(slot_hit, axis=1)
    home_shift = (group_id - own_request // max_requests) % n_grp
    own_state = jnp.take(
        every_group, home_shift * max_requests + own_request % max_requests, axis=0
    )
    merged = (own_state[..., 0], own_state[..., 1], own_state[..., 2:])
    own_query = slot_query[0].reshape(slot_count, layer_count, local_heads, head_size)
    own_kv = slot_new_kv[0].reshape(slot_count, layer_count, 2, local_heads, head_size)
    result = finish_slots(merged, own_query, own_kv, own_alive, scale_factor)
    return result.reshape(slot_count, layer_count, local_heads * head_size)


def per_device(
    stretch_in,
    norm_gain,
    w_qkv,
    w_out,
    prompt_cache,
    prompt_len,
    req_count,
    req_map,
    prefix_len,
    slot_query,
    slot_new_kv,
):
    group_id = lax.axis_index("grp")
    block_id = lax.axis_index("req")
    tensor_id = lax.axis_index("tp")
    replica_id = lax.axis_index(("grp", "req"))
    n_tp = lax.axis_size("tp")
    n_req = lax.axis_size("req")
    n_grp = lax.axis_size("grp")
    stretch_rows = stretch_in.shape[1]
    local_width = stretch_in.shape[2]
    tensor_width = local_width * n_tp
    head_size = HD
    local_heads = local_width // head_size
    cache_rows = prompt_cache.shape[3]
    layer_count = prompt_cache.shape[1]
    slot_count = slot_query.shape[1]
    scale_factor = head_size ** (-0.5)
    length = lax.dynamic_index_in_dim(prompt_len, group_id, 0, keepdims=False)

    rows_in = stretch_in[0]
    row_pieces = gather_shifts(rows_in, "tp", n_tp)
    full_rows = jnp.zeros((stretch_rows, tensor_width), rows_in.dtype)
    for shift, piece in enumerate(row_pieces):
        source = (tensor_id - shift) % n_tp
        full_rows = lax.dynamic_update_slice_in_dim(full_rows, piece, source * local_width, 1)
    widened = full_rows.astype(jnp.float32)
    mean_square = jnp.mean(widened * widened, axis=1, keepdims=True)
    normed = (widened * lax.rsqrt(mean_square + NORM_EPS) * norm_gain.astype(jnp.float32)).astype(
        jnp.bfloat16
    )

    qkv_cols = w_qkv.shape[1] * w_qkv.shape[2]
    both_weights = jnp.concatenate(
        [w_qkv.reshape(w_qkv.shape[0], qkv_cols), jnp.transpose(w_out)], axis=1
    )
    both_weights = lax.all_gather(both_weights, ("grp", "req"), axis=0, tiled=True)
    weight_piece = both_weights[:, :qkv_cols]
    out_weight_t = both_weights[:, qkv_cols:]
    merged_group = decode_slots(
        block_id, group_id, replica_id, n_req, n_grp, local_heads, head_size, scale_factor,
        prompt_cache, req_count, req_map, prefix_len, slot_query, slot_new_kv,
    )
    normed, merged_group = lax.optimization_barrier((normed, merged_group))

    projected = jnp.dot(normed, weight_piece, preferred_element_type=jnp.float32)
    projected = projected.reshape(stretch_rows, 3, local_heads, head_size)
    query_pos = block_id * stretch_rows + jnp.arange(stretch_rows, dtype=jnp.int32)
    cosine, sine_table = rope_angles(length + query_pos, head_size)
    queries = rotate_pairs(projected[:, 0], cosine, sine_table).astype(jnp.bfloat16)
    new_keys = rotate_pairs(projected[:, 1], cosine, sine_table).astype(jnp.bfloat16)
    new_values = projected[:, 2].astype(jnp.bfloat16)
    fresh_kv = jnp.stack(
        [
            new_keys.reshape(stretch_rows, local_width),
            new_values.reshape(stretch_rows, local_width),
        ],
        axis=0,
    )
    local_kv = jnp.concatenate([prompt_cache[0, 0], fresh_kv], axis=1)
    block_span = cache_rows + stretch_rows

    def attend_rows(carry, kv_piece, source):
        row_peak, totals, accumulated = carry
        piece_rows = kv_piece.shape[1]
        offset = jnp.arange(piece_rows, dtype=jnp.int32)
        from_cache = offset < cache_rows
        cache_pos = source * cache_rows + offset
        stretch_pos = source * stretch_rows + offset - cache_rows
        allowed = jnp.where(
            from_cache[None, :],
            cache_pos[None, :] < length,
            stretch_pos[None, :] <= query_pos[:, None],
        )
        piece_keys = kv_piece[0].reshape(piece_rows, local_heads, head_size)
        piece_values = kv_piece[1].reshape(piece_rows, local_heads, head_size)
        scores = (
            jnp.einsum("qhe,khe->hqk", queries, piece_keys, preferred_element_type=jnp.float32)
            * scale_factor
        )
        key_gate = allowed[None]
        masked = jnp.where(key_gate, scores, NEG_FLOOR)
        new_peak = jnp.maximum(row_peak, jnp.max(masked, axis=2))
        shrink = jnp.exp(row_peak - new_peak)
        weights = jnp.where(key_gate, jnp.exp(masked - new_peak[..., None]), 0.0)
        totals = totals * shrink + jnp.sum(weights, axis=2)
        update = jnp.einsum(
            "hqk,khe->qhe",
            weights.astype(jnp.bfloat16),
            piece_values,
            preferred_element_type=jnp.float32,
        )
        accumulated = accumulated * jnp.transpose(shrink)[:, :, None] + update
        return (new_peak, totals, accumulated)

    state = (
        jnp.full((local_heads, stretch_rows), NEG_FLOOR, jnp.float32),
        jnp.zeros((local_heads, stretch_rows), jnp.float32),
        jnp.zeros((stretch_rows, local_heads, head_size), jnp.float32),
    )
    chip_swap = [(i, i ^ 2) for i in range(n_req)]
    upward = [(i, i ^ 2) for i in range(n_req) if i < (i ^ 2)]
    half_rows = stretch_rows // 2
    partner_cache = lax.ppermute(prompt_cache[0, 0], "req", chip_swap)
    partner_low = lax.ppermute(fresh_kv[:, :half_rows], "req", upward)
    partner_high = lax.ppermute(fresh_kv[:, half_rows:], "req", upward)
    partner_kv = jnp.concatenate([partner_cache, partner_low, partner_high], axis=1)
    core_pair = jnp.stack([local_kv, partner_kv], axis=0)
    sibling_kv = lax.ppermute(core_pair, "req", [(i, i ^ 1) for i in range(n_req)])
    state = attend_rows(state, local_kv, block_id)
    remote_kv = jnp.concatenate([partner_kv[None], sibling_kv], axis=0)
    remote_xor = jnp.array([2, 1, 3], dtype=jnp.int32)

    def remote_block(step, inner_state):
        piece = lax.dynamic_index_in_dim(remote_kv, step, 0, keepdims=False)
        return attend_rows(inner_state, piece, jnp.bitwise_xor(block_id, remote_xor[step]))

    state = lax.fori_loop(0, n_req - 1, remote_block, state)
    row_peak, totals, accumulated = state
    attended = (
        (accumulated / jnp.transpose(totals)[:, :, None])
        .astype(jnp.bfloat16)
        .reshape(stretch_rows, local_width)
    )
    attended, merged_group = lax.optimization_barrier((attended, merged_group))
    result = finish_decode(
        merged_group, group_id, replica_id, n_grp, local_heads, head_size, scale_factor,
        prompt_cache, req_count, req_map, slot_query, slot_new_kv,
    )
    branch = None
    for shift in range(n_tp):
        target = (tensor_id + shift) % n_tp
        weight_block = lax.dynamic_slice_in_dim(out_weight_t, target * local_width, local_width, 0)
        product = lax.dot_general(
            attended,
            weight_block,
            (((1,), (1,)), ((), ())),
            preferred_element_type=jnp.float32,
        ).astype(jnp.bfloat16)
        if shift:
            product = lax.ppermute(
                product, "tp", [(i, (i + shift) % n_tp) for i in range(n_tp)]
            )
        term = product.astype(jnp.float32)
        branch = term if branch is None else branch + term
    branch = branch.astype(jnp.bfloat16)

    return (branch[None], result[None])


def solution(mesh):
    placed = (
        P("grp", "req", "tp"),
        P(),
        P(("grp", "req"), None, "tp"),
        P("tp", ("grp", "req")),
        P("grp", None, None, "req", "tp"),
        P(),
        P(),
        P(),
        P(),
        P(("grp", "req"), None, None, "tp"),
        P(("grp", "req"), None, None, None, "tp"),
    )
    return jax.shard_map(
        per_device,
        mesh=mesh,
        in_specs=placed,
        out_specs=(P("grp", "req", "tp"), P(("grp", "req"), None, None, "tp")),
        check_vma=False,
    )
```

```python
import jax
import jax.numpy as jnp
from jax import lax
from jax.sharding import PartitionSpec as P

HD = 96


NEG_FLOOR = -1e30
NORM_EPS = 1e-05
ROPE_BASE = 10000.0


def rope_angles(positions, head_size):
    half_size = head_size // 2
    freqs = ROPE_BASE ** (-(jnp.arange(half_size, dtype=jnp.float32) * 2.0 / head_size))
    angles = positions.astype(jnp.float32)[:, None] * freqs[None, :]
    return (jnp.cos(angles), jnp.sin(angles))


def rotate_pairs(values, cosine, sine_table):
    half_size = values.shape[-1] // 2
    first_half = values[..., :half_size]
    second_half = values[..., half_size:]
    cos_b = cosine[:, None, :]
    sin_b = sine_table[:, None, :]
    return jnp.concatenate(
        [first_half * cos_b - second_half * sin_b, second_half * cos_b + first_half * sin_b],
        axis=-1,
    )


def exact_round(values):
    return lax.optimization_barrier(values.astype(jnp.bfloat16)).astype(jnp.float32)


def cache_partial(queries, cache_keys, cache_values, allowed, scale_factor):
    scores = (
        jnp.einsum("slhe,lkhe->slhk", queries, cache_keys, preferred_element_type=jnp.float32)
        * scale_factor
    )
    key_gate = allowed[:, None, None, :]
    masked = jnp.where(key_gate, scores, NEG_FLOOR)
    row_peak = jnp.max(masked, axis=3)
    weights = jnp.where(key_gate, jnp.exp(masked - row_peak[..., None]), 0.0)
    totals = jnp.sum(weights, axis=3)
    accumulated = jnp.einsum(
        "slhk,lkhe->slhe",
        weights.astype(jnp.bfloat16),
        cache_values,
        preferred_element_type=jnp.float32,
    )
    return (row_peak, totals, accumulated)


def finish_slots(merged, own_query, own_kv, own_alive, scale_factor):
    row_peak, totals, accumulated = merged
    own_key = own_kv[:, :, 0]
    own_value = own_kv[:, :, 1]
    own_score = (
        jnp.einsum("slhe,slhe->slh", own_query, own_key, preferred_element_type=jnp.float32)
        * scale_factor
    )
    new_peak = jnp.maximum(row_peak, own_score)
    shrink = jnp.exp(row_peak - new_peak)
    own_weight = jnp.exp(own_score - new_peak)
    new_total = totals * shrink + own_weight
    mixed = accumulated * shrink[..., None] + exact_round(own_weight)[..., None] * own_value.astype(
        jnp.float32
    )
    result = mixed / new_total[..., None]
    result = jnp.where(own_alive[:, None, None, None], result, 0.0)
    return result.astype(jnp.bfloat16)


def gather_shifts(value, axis, count):
    pieces = [value]
    for shift in range(1, count):
        pieces.append(
            lax.ppermute(value, axis, [(i, (i + shift) % count) for i in range(count)])
        )
    return pieces


def decode_slots(
    block_id, group_id, replica_id, n_req, n_grp, local_heads, head_size, scale_factor,
    prompt_cache, req_count, req_map, prefix_len, slot_query, slot_new_kv,
):
    cache_rows = prompt_cache.shape[3]
    layer_count = prompt_cache.shape[1]
    slot_count = slot_query.shape[1]
    group_total, max_requests = req_map.shape
    flat_count = group_total * max_requests
    request_ids = jnp.arange(flat_count, dtype=jnp.int32)
    group_of = request_ids // max_requests
    count_of = jnp.sum(
        jnp.where(
            group_of[:, None] == jnp.arange(group_total, dtype=jnp.int32)[None, :],
            req_count[None, :],
            0,
        ),
        axis=1,
    )
    request_live = request_ids % max_requests < count_of
    flat_map = req_map.reshape(flat_count)
    earlier = (
        (flat_map[None, :] == flat_map[:, None])
        & request_live[None, :]
        & (request_ids[None, :] < request_ids[:, None])
    )
    order_rank = jnp.sum(earlier.astype(jnp.int32), axis=1)
    slot_of = jnp.where(request_live, flat_map * slot_count + order_rank, 0)
    prefix_flat = prefix_len.reshape(flat_count)
    first_request = group_id * max_requests
    mine_live = lax.dynamic_slice_in_dim(request_live, first_request, max_requests, 0)
    mine_slot = lax.dynamic_slice_in_dim(slot_of, first_request, max_requests, 0)
    mine_prefix = lax.dynamic_slice_in_dim(prefix_flat, first_request, max_requests, 0)
    by_block = jnp.concatenate(gather_shifts(slot_query[0], "req", n_req), axis=0)
    all_queries = jnp.concatenate(gather_shifts(by_block, "grp", n_grp), axis=0)
    home_replica = mine_slot // slot_count
    query_row = (
        ((group_id - home_replica // n_req) % n_grp) * (n_req * slot_count)
        + ((block_id - home_replica % n_req) % n_req) * slot_count
        + mine_slot % slot_count
    )
    picked = jnp.take(all_queries, query_row, axis=0).reshape(
        max_requests, layer_count, local_heads, head_size
    )
    cache_keys = prompt_cache[0, :, 0].reshape(layer_count, cache_rows, local_heads, head_size)
    cache_values = prompt_cache[0, :, 1].reshape(layer_count, cache_rows, local_heads, head_size)
    cache_pos = block_id * cache_rows + jnp.arange(cache_rows, dtype=jnp.int32)
    allowed = mine_live[:, None] & (cache_pos[None, :] < mine_prefix[:, None])
    part_peak, part_total, part_accum = cache_partial(
        picked, cache_keys, cache_values, allowed, scale_factor
    )
    packed = jnp.concatenate([part_peak[..., None], part_total[..., None], part_accum], axis=-1)
    block_parts = jnp.stack(gather_shifts(packed, "req", n_req), axis=0)
    peaks = block_parts[..., 0]
    group_peak = jnp.max(peaks, axis=0)
    factor = jnp.exp(peaks - group_peak[None])
    group_total_w = jnp.sum(block_parts[..., 1] * factor, axis=0)
    group_accum = jnp.sum(block_parts[..., 2:] * factor[..., None], axis=0)
    merged_group = jnp.concatenate(
        [group_peak[..., None], group_total_w[..., None], group_accum], axis=-1
    )
    return merged_group


def finish_decode(
    merged_group, group_id, replica_id, n_grp, local_heads, head_size, scale_factor,
    prompt_cache, req_count, req_map, slot_query, slot_new_kv,
):
    layer_count = prompt_cache.shape[1]
    slot_count = slot_query.shape[1]
    group_total, max_requests = req_map.shape
    flat_count = group_total * max_requests
    request_ids = jnp.arange(flat_count, dtype=jnp.int32)
    group_of = request_ids // max_requests
    count_of = jnp.sum(
        jnp.where(
            group_of[:, None] == jnp.arange(group_total, dtype=jnp.int32)[None, :],
            req_count[None, :],
            0,
        ),
        axis=1,
    )
    request_live = request_ids % max_requests < count_of
    flat_map = req_map.reshape(flat_count)
    earlier = (
        (flat_map[None, :] == flat_map[:, None])
        & request_live[None, :]
        & (request_ids[None, :] < request_ids[:, None])
    )
    order_rank = jnp.sum(earlier.astype(jnp.int32), axis=1)
    every_group = jnp.concatenate(gather_shifts(merged_group, "grp", n_grp), axis=0)
    slot_hit = (
        request_live[None, :]
        & (flat_map[None, :] == replica_id)
        & (order_rank[None, :] == jnp.arange(slot_count, dtype=jnp.int32)[:, None])
    )
    own_request = jnp.sum(jnp.where(slot_hit, request_ids[None, :], 0), axis=1)
    own_alive = jnp.any(slot_hit, axis=1)
    home_shift = (group_id - own_request // max_requests) % n_grp
    own_state = jnp.take(
        every_group, home_shift * max_requests + own_request % max_requests, axis=0
    )
    merged = (own_state[..., 0], own_state[..., 1], own_state[..., 2:])
    own_query = slot_query[0].reshape(slot_count, layer_count, local_heads, head_size)
    own_kv = slot_new_kv[0].reshape(slot_count, layer_count, 2, local_heads, head_size)
    result = finish_slots(merged, own_query, own_kv, own_alive, scale_factor)
    return result.reshape(slot_count, layer_count, local_heads * head_size)


def per_device(
    stretch_in,
    norm_gain,
    w_qkv,
    w_out,
    prompt_cache,
    prompt_len,
    req_count,
    req_map,
    prefix_len,
    slot_query,
    slot_new_kv,
):
    group_id = lax.axis_index("grp")
    block_id = lax.axis_index("req")
    tensor_id = lax.axis_index("tp")
    replica_id = lax.axis_index(("grp", "req"))
    n_tp = lax.axis_size("tp")
    n_req = lax.axis_size("req")
    n_grp = lax.axis_size("grp")
    stretch_rows = stretch_in.shape[1]
    local_width = stretch_in.shape[2]
    tensor_width = local_width * n_tp
    head_size = HD
    local_heads = local_width // head_size
    cache_rows = prompt_cache.shape[3]
    layer_count = prompt_cache.shape[1]
    slot_count = slot_query.shape[1]
    scale_factor = head_size ** (-0.5)
    length = lax.dynamic_index_in_dim(prompt_len, group_id, 0, keepdims=False)

    rows_in = stretch_in[0]
    row_pieces = gather_shifts(rows_in, "tp", n_tp)
    full_rows = jnp.zeros((stretch_rows, tensor_width), rows_in.dtype)
    for shift, piece in enumerate(row_pieces):
        source = (tensor_id - shift) % n_tp
        full_rows = lax.dynamic_update_slice_in_dim(full_rows, piece, source * local_width, 1)
    widened = full_rows.astype(jnp.float32)
    mean_square = jnp.mean(widened * widened, axis=1, keepdims=True)
    normed = (widened * lax.rsqrt(mean_square + NORM_EPS) * norm_gain.astype(jnp.float32)).astype(
        jnp.bfloat16
    )

    qkv_cols = w_qkv.shape[1] * w_qkv.shape[2]
    both_weights = jnp.concatenate(
        [w_qkv.reshape(w_qkv.shape[0], qkv_cols), jnp.transpose(w_out)], axis=1
    )
    both_weights = lax.all_gather(both_weights, ("grp", "req"), axis=0, tiled=True)
    weight_piece = both_weights[:, :qkv_cols]
    out_weight_t = both_weights[:, qkv_cols:]
    merged_group = decode_slots(
        block_id, group_id, replica_id, n_req, n_grp, local_heads, head_size, scale_factor,
        prompt_cache, req_count, req_map, prefix_len, slot_query, slot_new_kv,
    )
    normed, merged_group = lax.optimization_barrier((normed, merged_group))

    projected = jnp.dot(normed, weight_piece, preferred_element_type=jnp.float32)
    projected = projected.reshape(stretch_rows, 3, local_heads, head_size)
    query_pos = block_id * stretch_rows + jnp.arange(stretch_rows, dtype=jnp.int32)
    cosine, sine_table = rope_angles(length + query_pos, head_size)
    queries = rotate_pairs(projected[:, 0], cosine, sine_table).astype(jnp.bfloat16)
    new_keys = rotate_pairs(projected[:, 1], cosine, sine_table).astype(jnp.bfloat16)
    new_values = projected[:, 2].astype(jnp.bfloat16)
    fresh_kv = jnp.stack(
        [
            new_keys.reshape(stretch_rows, local_width),
            new_values.reshape(stretch_rows, local_width),
        ],
        axis=0,
    )
    local_kv = jnp.concatenate([prompt_cache[0, 0], fresh_kv], axis=1)
    block_span = cache_rows + stretch_rows

    def attend_rows(carry, kv_piece, source):
        row_peak, totals, accumulated = carry
        piece_rows = kv_piece.shape[1]
        offset = jnp.arange(piece_rows, dtype=jnp.int32)
        from_cache = offset < cache_rows
        cache_pos = source * cache_rows + offset
        stretch_pos = source * stretch_rows + offset - cache_rows
        allowed = jnp.where(
            from_cache[None, :],
            cache_pos[None, :] < length,
            stretch_pos[None, :] <= query_pos[:, None],
        )
        piece_keys = kv_piece[0].reshape(piece_rows, local_heads, head_size)
        piece_values = kv_piece[1].reshape(piece_rows, local_heads, head_size)
        scores = (
            jnp.einsum("qhe,khe->hqk", queries, piece_keys, preferred_element_type=jnp.float32)
            * scale_factor
        )
        key_gate = allowed[None]
        masked = jnp.where(key_gate, scores, NEG_FLOOR)
        new_peak = jnp.maximum(row_peak, jnp.max(masked, axis=2))
        shrink = jnp.exp(row_peak - new_peak)
        weights = jnp.where(key_gate, jnp.exp(masked - new_peak[..., None]), 0.0)
        totals = totals * shrink + jnp.sum(weights, axis=2)
        update = jnp.einsum(
            "hqk,khe->qhe",
            weights.astype(jnp.bfloat16),
            piece_values,
            preferred_element_type=jnp.float32,
        )
        accumulated = accumulated * jnp.transpose(shrink)[:, :, None] + update
        return (new_peak, totals, accumulated)

    state = (
        jnp.full((local_heads, stretch_rows), NEG_FLOOR, jnp.float32),
        jnp.zeros((local_heads, stretch_rows), jnp.float32),
        jnp.zeros((stretch_rows, local_heads, head_size), jnp.float32),
    )
    chip_swap = [(i, i ^ 2) for i in range(n_req)]
    upward = [(i, i ^ 2) for i in range(n_req) if i < (i ^ 2)]
    half_rows = stretch_rows // 2
    partner_cache = lax.ppermute(prompt_cache[0, 0], "req", chip_swap)
    partner_low = lax.ppermute(fresh_kv[:, :half_rows], "req", upward)
    partner_high = lax.ppermute(fresh_kv[:, half_rows:], "req", upward)
    partner_kv = jnp.concatenate([partner_cache, partner_low, partner_high], axis=1)
    core_pair = jnp.stack([local_kv, partner_kv], axis=0)
    sibling_kv = lax.ppermute(core_pair, "req", [(i, i ^ 1) for i in range(n_req)])
    state = attend_rows(state, local_kv, block_id)
    remote_kv = jnp.concatenate([partner_kv[None], sibling_kv], axis=0)
    remote_xor = jnp.array([2, 1, 3], dtype=jnp.int32)

    def remote_block(step, inner_state):
        piece = lax.dynamic_index_in_dim(remote_kv, step, 0, keepdims=False)
        return attend_rows(inner_state, piece, jnp.bitwise_xor(block_id, remote_xor[step]))

    state = lax.fori_loop(0, n_req - 1, remote_block, state)
    row_peak, totals, accumulated = state
    attended = (
        (accumulated / jnp.transpose(totals)[:, :, None])
        .astype(jnp.bfloat16)
        .reshape(stretch_rows, local_width)
    )
    branch = None
    for shift in range(n_tp):
        target = (tensor_id + shift) % n_tp
        weight_block = lax.dynamic_slice_in_dim(out_weight_t, target * local_width, local_width, 0)
        product = lax.dot_general(
            attended,
            weight_block,
            (((1,), (1,)), ((), ())),
            preferred_element_type=jnp.float32,
        ).astype(jnp.bfloat16)
        if shift:
            product = lax.ppermute(
                product, "tp", [(i, (i + shift) % n_tp) for i in range(n_tp)]
            )
        if shift == 1:
            product, merged_group = lax.optimization_barrier((product, merged_group))
        term = product.astype(jnp.float32)
        branch = term if branch is None else branch + term
    branch = branch.astype(jnp.bfloat16)
    result = finish_decode(
        merged_group, group_id, replica_id, n_grp, local_heads, head_size, scale_factor,
        prompt_cache, req_count, req_map, slot_query, slot_new_kv,
    )

    return (branch[None], result[None])


def solution(mesh):
    placed = (
        P("grp", "req", "tp"),
        P(),
        P(("grp", "req"), None, "tp"),
        P("tp", ("grp", "req")),
        P("grp", None, None, "req", "tp"),
        P(),
        P(),
        P(),
        P(),
        P(("grp", "req"), None, None, "tp"),
        P(("grp", "req"), None, None, None, "tp"),
    )
    return jax.shard_map(
        per_device,
        mesh=mesh,
        in_specs=placed,
        out_specs=(P("grp", "req", "tp"), P(("grp", "req"), None, None, "tp")),
        check_vma=False,
    )
```

```python
import jax
import jax.numpy as jnp
from jax import lax
from jax.sharding import PartitionSpec as P

HD = 96


NEG_FLOOR = -1e30
NORM_EPS = 1e-05
ROPE_BASE = 10000.0


def rope_angles(positions, head_size):
    half_size = head_size // 2
    freqs = ROPE_BASE ** (-(jnp.arange(half_size, dtype=jnp.float32) * 2.0 / head_size))
    angles = positions.astype(jnp.float32)[:, None] * freqs[None, :]
    return (jnp.cos(angles), jnp.sin(angles))


def rotate_pairs(values, cosine, sine_table):
    half_size = values.shape[-1] // 2
    first_half = values[..., :half_size]
    second_half = values[..., half_size:]
    cos_b = cosine[:, None, :]
    sin_b = sine_table[:, None, :]
    return jnp.concatenate(
        [first_half * cos_b - second_half * sin_b, second_half * cos_b + first_half * sin_b],
        axis=-1,
    )


def exact_round(values):
    return lax.optimization_barrier(values.astype(jnp.bfloat16)).astype(jnp.float32)


def cache_partial(queries, cache_keys, cache_values, allowed, scale_factor):
    scores = (
        jnp.einsum("slhe,lkhe->slhk", queries, cache_keys, preferred_element_type=jnp.float32)
        * scale_factor
    )
    key_gate = allowed[:, None, None, :]
    masked = jnp.where(key_gate, scores, NEG_FLOOR)
    row_peak = jnp.max(masked, axis=3)
    weights = jnp.where(key_gate, jnp.exp(masked - row_peak[..., None]), 0.0)
    totals = jnp.sum(weights, axis=3)
    accumulated = jnp.einsum(
        "slhk,lkhe->slhe",
        weights.astype(jnp.bfloat16),
        cache_values,
        preferred_element_type=jnp.float32,
    )
    return (row_peak, totals, accumulated)


def finish_slots(merged, own_query, own_kv, own_alive, scale_factor):
    row_peak, totals, accumulated = merged
    own_key = own_kv[:, :, 0]
    own_value = own_kv[:, :, 1]
    own_score = (
        jnp.einsum("slhe,slhe->slh", own_query, own_key, preferred_element_type=jnp.float32)
        * scale_factor
    )
    new_peak = jnp.maximum(row_peak, own_score)
    shrink = jnp.exp(row_peak - new_peak)
    own_weight = jnp.exp(own_score - new_peak)
    new_total = totals * shrink + own_weight
    mixed = accumulated * shrink[..., None] + exact_round(own_weight)[..., None] * own_value.astype(
        jnp.float32
    )
    result = mixed / new_total[..., None]
    result = jnp.where(own_alive[:, None, None, None], result, 0.0)
    return result.astype(jnp.bfloat16)


def gather_shifts(value, axis, count):
    pieces = [value]
    for shift in range(1, count):
        pieces.append(
            lax.ppermute(value, axis, [(i, (i + shift) % count) for i in range(count)])
        )
    return pieces


def decode_slots(
    block_id, group_id, n_req, n_grp, local_heads, head_size, scale_factor,
    prompt_cache, req_count, req_map, prefix_len, slot_query,
):
    cache_rows = prompt_cache.shape[3]
    layer_count = prompt_cache.shape[1]
    slot_count = slot_query.shape[1]
    group_total, max_requests = req_map.shape
    flat_count = group_total * max_requests
    request_ids = jnp.arange(flat_count, dtype=jnp.int32)
    group_of = request_ids // max_requests
    count_of = jnp.sum(
        jnp.where(
            group_of[:, None] == jnp.arange(group_total, dtype=jnp.int32)[None, :],
            req_count[None, :],
            0,
        ),
        axis=1,
    )
    request_live = request_ids % max_requests < count_of
    flat_map = req_map.reshape(flat_count)
    earlier = (
        (flat_map[None, :] == flat_map[:, None])
        & request_live[None, :]
        & (request_ids[None, :] < request_ids[:, None])
    )
    order_rank = jnp.sum(earlier.astype(jnp.int32), axis=1)
    slot_of = jnp.where(request_live, flat_map * slot_count + order_rank, 0)
    prefix_flat = prefix_len.reshape(flat_count)
    first_request = group_id * max_requests
    mine_live = lax.dynamic_slice_in_dim(request_live, first_request, max_requests, 0)
    mine_slot = lax.dynamic_slice_in_dim(slot_of, first_request, max_requests, 0)
    mine_prefix = lax.dynamic_slice_in_dim(prefix_flat, first_request, max_requests, 0)
    by_block = jnp.concatenate(gather_shifts(slot_query[0], "req", n_req), axis=0)
    all_queries = jnp.concatenate(gather_shifts(by_block, "grp", n_grp), axis=0)
    home_replica = mine_slot // slot_count
    query_row = (
        ((group_id - home_replica // n_req) % n_grp) * (n_req * slot_count)
        + ((block_id - home_replica % n_req) % n_req) * slot_count
        + mine_slot % slot_count
    )
    picked = jnp.take(all_queries, query_row, axis=0).reshape(
        max_requests, layer_count, local_heads, head_size
    )
    cache_keys = prompt_cache[0, :, 0].reshape(layer_count, cache_rows, local_heads, head_size)
    cache_values = prompt_cache[0, :, 1].reshape(layer_count, cache_rows, local_heads, head_size)
    cache_pos = block_id * cache_rows + jnp.arange(cache_rows, dtype=jnp.int32)
    allowed = mine_live[:, None] & (cache_pos[None, :] < mine_prefix[:, None])
    part_peak, part_total, part_accum = cache_partial(
        picked, cache_keys, cache_values, allowed, scale_factor
    )
    packed = jnp.concatenate([part_peak[..., None], part_total[..., None], part_accum], axis=-1)
    block_parts = jnp.stack(gather_shifts(packed, "req", n_req), axis=0)
    peaks = block_parts[..., 0]
    group_peak = jnp.max(peaks, axis=0)
    factor = jnp.exp(peaks - group_peak[None])
    group_total_w = jnp.sum(block_parts[..., 1] * factor, axis=0)
    group_accum = jnp.sum(block_parts[..., 2:] * factor[..., None], axis=0)
    merged_group = jnp.concatenate(
        [group_peak[..., None], group_total_w[..., None], group_accum], axis=-1
    )
    return merged_group


def finish_decode(
    merged_group, group_id, replica_id, n_grp, local_heads, head_size, scale_factor,
    prompt_cache, req_count, req_map, slot_query, slot_new_kv,
):
    layer_count = prompt_cache.shape[1]
    slot_count = slot_query.shape[1]
    group_total, max_requests = req_map.shape
    flat_count = group_total * max_requests
    request_ids = jnp.arange(flat_count, dtype=jnp.int32)
    group_of = request_ids // max_requests
    count_of = jnp.sum(
        jnp.where(
            group_of[:, None] == jnp.arange(group_total, dtype=jnp.int32)[None, :],
            req_count[None, :],
            0,
        ),
        axis=1,
    )
    request_live = request_ids % max_requests < count_of
    flat_map = req_map.reshape(flat_count)
    earlier = (
        (flat_map[None, :] == flat_map[:, None])
        & request_live[None, :]
        & (request_ids[None, :] < request_ids[:, None])
    )
    order_rank = jnp.sum(earlier.astype(jnp.int32), axis=1)
    every_group = jnp.concatenate(gather_shifts(merged_group, "grp", n_grp), axis=0)
    slot_hit = (
        request_live[None, :]
        & (flat_map[None, :] == replica_id)
        & (order_rank[None, :] == jnp.arange(slot_count, dtype=jnp.int32)[:, None])
    )
    own_request = jnp.sum(jnp.where(slot_hit, request_ids[None, :], 0), axis=1)
    own_alive = jnp.any(slot_hit, axis=1)
    home_shift = (group_id - own_request // max_requests) % n_grp
    own_state = jnp.take(
        every_group, home_shift * max_requests + own_request % max_requests, axis=0
    )
    merged = (own_state[..., 0], own_state[..., 1], own_state[..., 2:])
    own_query = slot_query[0].reshape(slot_count, layer_count, local_heads, head_size)
    own_kv = slot_new_kv[0].reshape(slot_count, layer_count, 2, local_heads, head_size)
    result = finish_slots(merged, own_query, own_kv, own_alive, scale_factor)
    return result.reshape(slot_count, layer_count, local_heads * head_size)


def per_device(
    stretch_in,
    norm_gain,
    w_qkv,
    w_out,
    prompt_cache,
    prompt_len,
    req_count,
    req_map,
    prefix_len,
    slot_query,
    slot_new_kv,
):
    group_id = lax.axis_index("grp")
    block_id = lax.axis_index("req")
    tensor_id = lax.axis_index("tp")
    replica_id = lax.axis_index(("grp", "req"))
    n_tp = lax.axis_size("tp")
    n_req = lax.axis_size("req")
    n_grp = lax.axis_size("grp")
    stretch_rows = stretch_in.shape[1]
    local_width = stretch_in.shape[2]
    tensor_width = local_width * n_tp
    head_size = HD
    local_heads = local_width // head_size
    cache_rows = prompt_cache.shape[3]
    scale_factor = head_size ** (-0.5)
    length = lax.dynamic_index_in_dim(prompt_len, group_id, 0, keepdims=False)

    rows_in = stretch_in[0]
    row_pieces = gather_shifts(rows_in, "tp", n_tp)
    full_rows = jnp.zeros((stretch_rows, tensor_width), rows_in.dtype)
    for shift, piece in enumerate(row_pieces):
        source = (tensor_id - shift) % n_tp
        full_rows = lax.dynamic_update_slice_in_dim(full_rows, piece, source * local_width, 1)
    widened = full_rows.astype(jnp.float32)
    mean_square = jnp.mean(widened * widened, axis=1, keepdims=True)
    normed = (widened * lax.rsqrt(mean_square + NORM_EPS) * norm_gain.astype(jnp.float32)).astype(
        jnp.bfloat16
    )

    qkv_cols = w_qkv.shape[1] * w_qkv.shape[2]
    both_weights = jnp.concatenate(
        [w_qkv.reshape(w_qkv.shape[0], qkv_cols), jnp.transpose(w_out)], axis=1
    )
    both_weights = lax.all_gather(both_weights, ("grp", "req"), axis=0, tiled=True)
    weight_piece = both_weights[:, :qkv_cols]
    out_weight_t = both_weights[:, qkv_cols:]
    merged_group = decode_slots(
        block_id, group_id, n_req, n_grp, local_heads, head_size, scale_factor,
        prompt_cache, req_count, req_map, prefix_len, slot_query,
    )
    normed, merged_group = lax.optimization_barrier((normed, merged_group))

    projected = jnp.dot(normed, weight_piece, preferred_element_type=jnp.float32)
    projected = projected.reshape(stretch_rows, 3, local_heads, head_size)
    query_pos = block_id * stretch_rows + jnp.arange(stretch_rows, dtype=jnp.int32)
    cosine, sine_table = rope_angles(length + query_pos, head_size)
    queries = rotate_pairs(projected[:, 0], cosine, sine_table).astype(jnp.bfloat16)
    new_keys = rotate_pairs(projected[:, 1], cosine, sine_table).astype(jnp.bfloat16)
    new_values = projected[:, 2].astype(jnp.bfloat16)
    fresh_kv = jnp.stack(
        [
            new_keys.reshape(stretch_rows, local_width),
            new_values.reshape(stretch_rows, local_width),
        ],
        axis=0,
    )
    local_kv = jnp.concatenate([prompt_cache[0, 0], fresh_kv], axis=1)

    def attend_rows(carry, kv_piece, source):
        row_peak, totals, accumulated = carry
        piece_rows = kv_piece.shape[1]
        offset = jnp.arange(piece_rows, dtype=jnp.int32)
        from_cache = offset < cache_rows
        cache_pos = source * cache_rows + offset
        stretch_pos = source * stretch_rows + offset - cache_rows
        allowed = jnp.where(
            from_cache[None, :],
            cache_pos[None, :] < length,
            stretch_pos[None, :] <= query_pos[:, None],
        )
        piece_keys = kv_piece[0].reshape(piece_rows, local_heads, head_size)
        piece_values = kv_piece[1].reshape(piece_rows, local_heads, head_size)
        scores = (
            jnp.einsum("qhe,khe->hqk", queries, piece_keys, preferred_element_type=jnp.float32)
            * scale_factor
        )
        key_gate = allowed[None]
        masked = jnp.where(key_gate, scores, NEG_FLOOR)
        new_peak = jnp.maximum(row_peak, jnp.max(masked, axis=2))
        shrink = jnp.exp(row_peak - new_peak)
        weights = jnp.where(key_gate, jnp.exp(masked - new_peak[..., None]), 0.0)
        totals = totals * shrink + jnp.sum(weights, axis=2)
        update = jnp.einsum(
            "hqk,khe->qhe",
            weights.astype(jnp.bfloat16),
            piece_values,
            preferred_element_type=jnp.float32,
        )
        accumulated = accumulated * jnp.transpose(shrink)[:, :, None] + update
        return (new_peak, totals, accumulated)

    state = (
        jnp.full((local_heads, stretch_rows), NEG_FLOOR, jnp.float32),
        jnp.zeros((local_heads, stretch_rows), jnp.float32),
        jnp.zeros((stretch_rows, local_heads, head_size), jnp.float32),
    )
    chip_swap = [(i, i ^ 2) for i in range(n_req)]
    upward = [(i, i ^ 2) for i in range(n_req) if i < (i ^ 2)]
    half_rows = stretch_rows // 2
    partner_cache = lax.ppermute(prompt_cache[0, 0], "req", chip_swap)
    partner_low = lax.ppermute(fresh_kv[:, :half_rows], "req", upward)
    partner_high = lax.ppermute(fresh_kv[:, half_rows:], "req", upward)
    partner_kv = jnp.concatenate([partner_cache, partner_low, partner_high], axis=1)
    core_pair = jnp.stack([local_kv, partner_kv], axis=0)
    sibling_kv = lax.ppermute(core_pair, "req", [(i, i ^ 1) for i in range(n_req)])
    state = attend_rows(state, local_kv, block_id)
    remote_kv = jnp.concatenate([partner_kv[None], sibling_kv], axis=0)
    remote_xor = jnp.array([2, 1, 3], dtype=jnp.int32)

    def remote_block(step, inner_state):
        piece = lax.dynamic_index_in_dim(remote_kv, step, 0, keepdims=False)
        return attend_rows(inner_state, piece, jnp.bitwise_xor(block_id, remote_xor[step]))

    state = lax.fori_loop(0, n_req - 1, remote_block, state)
    _, totals, accumulated = state
    attended = (
        (accumulated / jnp.transpose(totals)[:, :, None])
        .astype(jnp.bfloat16)
        .reshape(stretch_rows, local_width)
    )
    branch = None
    for shift in range(n_tp):
        target = (tensor_id + shift) % n_tp
        weight_block = lax.dynamic_slice_in_dim(out_weight_t, target * local_width, local_width, 0)
        product = lax.dot_general(
            attended,
            weight_block,
            (((1,), (1,)), ((), ())),
            preferred_element_type=jnp.float32,
        ).astype(jnp.bfloat16)
        if shift:
            product = lax.ppermute(
                product, "tp", [(i, (i + shift) % n_tp) for i in range(n_tp)]
            )
        if shift == 1:
            product, merged_group = lax.optimization_barrier((product, merged_group))
        term = product.astype(jnp.float32)
        branch = term if branch is None else branch + term
    branch = branch.astype(jnp.bfloat16)
    result = finish_decode(
        merged_group, group_id, replica_id, n_grp, local_heads, head_size, scale_factor,
        prompt_cache, req_count, req_map, slot_query, slot_new_kv,
    )

    return (branch[None], result[None])


def solution(mesh):
    placed = (
        P("grp", "req", "tp"),
        P(),
        P(("grp", "req"), None, "tp"),
        P("tp", ("grp", "req")),
        P("grp", None, None, "req", "tp"),
        P(),
        P(),
        P(),
        P(),
        P(("grp", "req"), None, None, "tp"),
        P(("grp", "req"), None, None, None, "tp"),
    )

    return jax.shard_map(
        per_device,
        mesh=mesh,
        in_specs=placed,
        out_specs=(P("grp", "req", "tp"), P(("grp", "req"), None, None, "tp")),
        check_vma=False,
    )
```

```python
import jax
import jax.numpy as jnp
from jax import lax
from jax.sharding import PartitionSpec as P

HD = 96


NEG_FLOOR = -1e30
NORM_EPS = 1e-05
ROPE_BASE = 10000.0


def rope_angles(positions, head_size):
    half_size = head_size // 2
    freqs = ROPE_BASE ** (-(jnp.arange(half_size, dtype=jnp.float32) * 2.0 / head_size))
    angles = positions.astype(jnp.float32)[:, None] * freqs[None, :]
    return (jnp.cos(angles), jnp.sin(angles))


def rotate_pairs(values, cosine, sine_table):
    half_size = values.shape[-1] // 2
    first_half = values[..., :half_size]
    second_half = values[..., half_size:]
    cos_b = cosine[:, None, :]
    sin_b = sine_table[:, None, :]
    return jnp.concatenate(
        [first_half * cos_b - second_half * sin_b, second_half * cos_b + first_half * sin_b],
        axis=-1,
    )


def exact_round(values):
    return lax.optimization_barrier(values.astype(jnp.bfloat16)).astype(jnp.float32)


def cache_partial(queries, cache_keys, cache_values, allowed, scale_factor):
    scores = (
        jnp.einsum("slhe,lkhe->slhk", queries, cache_keys, preferred_element_type=jnp.float32)
        * scale_factor
    )
    key_gate = allowed[:, None, None, :]
    masked = jnp.where(key_gate, scores, NEG_FLOOR)
    row_peak = jnp.max(masked, axis=3)
    weights = jnp.where(key_gate, jnp.exp(masked - row_peak[..., None]), 0.0)
    totals = jnp.sum(weights, axis=3)
    accumulated = jnp.einsum(
        "slhk,lkhe->slhe",
        weights.astype(jnp.bfloat16),
        cache_values,
        preferred_element_type=jnp.float32,
    )
    return (row_peak, totals, accumulated)


def finish_slots(merged, own_query, own_kv, own_alive, scale_factor):
    row_peak, totals, accumulated = merged
    own_key = own_kv[:, :, 0]
    own_value = own_kv[:, :, 1]
    own_score = (
        jnp.einsum("slhe,slhe->slh", own_query, own_key, preferred_element_type=jnp.float32)
        * scale_factor
    )
    new_peak = jnp.maximum(row_peak, own_score)
    shrink = jnp.exp(row_peak - new_peak)
    own_weight = jnp.exp(own_score - new_peak)
    new_total = totals * shrink + own_weight
    mixed = accumulated * shrink[..., None] + exact_round(own_weight)[..., None] * own_value.astype(
        jnp.float32
    )
    result = mixed / new_total[..., None]
    result = jnp.where(own_alive[:, None, None, None], result, 0.0)
    return result.astype(jnp.bfloat16)


def gather_shifts(value, axis, count):
    pieces = [value]
    for shift in range(1, count):
        pieces.append(
            lax.ppermute(value, axis, [(i, (i + shift) % count) for i in range(count)])
        )
    return pieces


def decode_slots(
    block_id, group_id, replica_id, n_req, n_grp, local_heads, head_size, scale_factor,
    prompt_cache, req_count, req_map, prefix_len, slot_query, slot_new_kv,
):
    cache_rows = prompt_cache.shape[3]
    layer_count = prompt_cache.shape[1]
    slot_count = slot_query.shape[1]
    group_total, max_requests = req_map.shape
    flat_count = group_total * max_requests
    request_ids = jnp.arange(flat_count, dtype=jnp.int32)
    group_of = request_ids // max_requests
    count_of = jnp.sum(
        jnp.where(
            group_of[:, None] == jnp.arange(group_total, dtype=jnp.int32)[None, :],
            req_count[None, :],
            0,
        ),
        axis=1,
    )
    request_live = request_ids % max_requests < count_of
    flat_map = req_map.reshape(flat_count)
    earlier = (
        (flat_map[None, :] == flat_map[:, None])
        & request_live[None, :]
        & (request_ids[None, :] < request_ids[:, None])
    )
    order_rank = jnp.sum(earlier.astype(jnp.int32), axis=1)
    slot_of = jnp.where(request_live, flat_map * slot_count + order_rank, 0)
    prefix_flat = prefix_len.reshape(flat_count)
    first_request = group_id * max_requests
    mine_live = lax.dynamic_slice_in_dim(request_live, first_request, max_requests, 0)
    mine_slot = lax.dynamic_slice_in_dim(slot_of, first_request, max_requests, 0)
    mine_prefix = lax.dynamic_slice_in_dim(prefix_flat, first_request, max_requests, 0)
    by_block = jnp.concatenate(gather_shifts(slot_query[0], "req", n_req), axis=0)
    all_queries = jnp.concatenate(gather_shifts(by_block, "grp", n_grp), axis=0)
    home_replica = mine_slot // slot_count
    query_row = (
        ((group_id - home_replica // n_req) % n_grp) * (n_req * slot_count)
        + ((block_id - home_replica % n_req) % n_req) * slot_count
        + mine_slot % slot_count
    )
    picked = jnp.take(all_queries, query_row, axis=0).reshape(
        max_requests, layer_count, local_heads, head_size
    )
    cache_keys = prompt_cache[0, :, 0].reshape(layer_count, cache_rows, local_heads, head_size)
    cache_values = prompt_cache[0, :, 1].reshape(layer_count, cache_rows, local_heads, head_size)
    cache_pos = block_id * cache_rows + jnp.arange(cache_rows, dtype=jnp.int32)
    allowed = mine_live[:, None] & (cache_pos[None, :] < mine_prefix[:, None])
    part_peak, part_total, part_accum = cache_partial(
        picked, cache_keys, cache_values, allowed, scale_factor
    )
    packed = jnp.concatenate([part_peak[..., None], part_total[..., None], part_accum], axis=-1)
    block_parts = jnp.stack(gather_shifts(packed, "req", n_req), axis=0)
    peaks = block_parts[..., 0]
    group_peak = jnp.max(peaks, axis=0)
    factor = jnp.exp(peaks - group_peak[None])
    group_total_w = jnp.sum(block_parts[..., 1] * factor, axis=0)
    group_accum = jnp.sum(block_parts[..., 2:] * factor[..., None], axis=0)
    merged_group = jnp.concatenate(
        [group_peak[..., None], group_total_w[..., None], group_accum], axis=-1
    )
    return merged_group


def finish_decode(
    merged_group, group_id, replica_id, n_grp, local_heads, head_size, scale_factor,
    prompt_cache, req_count, req_map, slot_query, slot_new_kv,
):
    layer_count = prompt_cache.shape[1]
    slot_count = slot_query.shape[1]
    group_total, max_requests = req_map.shape
    flat_count = group_total * max_requests
    request_ids = jnp.arange(flat_count, dtype=jnp.int32)
    group_of = request_ids // max_requests
    count_of = jnp.sum(
        jnp.where(
            group_of[:, None] == jnp.arange(group_total, dtype=jnp.int32)[None, :],
            req_count[None, :],
            0,
        ),
        axis=1,
    )
    request_live = request_ids % max_requests < count_of
    flat_map = req_map.reshape(flat_count)
    earlier = (
        (flat_map[None, :] == flat_map[:, None])
        & request_live[None, :]
        & (request_ids[None, :] < request_ids[:, None])
    )
    order_rank = jnp.sum(earlier.astype(jnp.int32), axis=1)
    every_group = jnp.concatenate(gather_shifts(merged_group, "grp", n_grp), axis=0)
    slot_hit = (
        request_live[None, :]
        & (flat_map[None, :] == replica_id)
        & (order_rank[None, :] == jnp.arange(slot_count, dtype=jnp.int32)[:, None])
    )
    own_request = jnp.sum(jnp.where(slot_hit, request_ids[None, :], 0), axis=1)
    own_alive = jnp.any(slot_hit, axis=1)
    home_shift = (group_id - own_request // max_requests) % n_grp
    own_state = jnp.take(
        every_group, home_shift * max_requests + own_request % max_requests, axis=0
    )
    merged = (own_state[..., 0], own_state[..., 1], own_state[..., 2:])
    own_query = slot_query[0].reshape(slot_count, layer_count, local_heads, head_size)
    own_kv = slot_new_kv[0].reshape(slot_count, layer_count, 2, local_heads, head_size)
    result = finish_slots(merged, own_query, own_kv, own_alive, scale_factor)
    return result.reshape(slot_count, layer_count, local_heads * head_size)


def per_device(
    stretch_in,
    norm_gain,
    w_qkv,
    w_out,
    prompt_cache,
    prompt_len,
    req_count,
    req_map,
    prefix_len,
    slot_query,
    slot_new_kv,
):
    group_id = lax.axis_index("grp")
    block_id = lax.axis_index("req")
    tensor_id = lax.axis_index("tp")
    replica_id = lax.axis_index(("grp", "req"))
    n_tp = lax.axis_size("tp")
    n_req = lax.axis_size("req")
    n_grp = lax.axis_size("grp")
    stretch_rows = stretch_in.shape[1]
    local_width = stretch_in.shape[2]
    tensor_width = local_width * n_tp
    head_size = HD
    local_heads = local_width // head_size
    cache_rows = prompt_cache.shape[3]
    layer_count = prompt_cache.shape[1]
    slot_count = slot_query.shape[1]
    scale_factor = head_size ** (-0.5)
    length = lax.dynamic_index_in_dim(prompt_len, group_id, 0, keepdims=False)

    rows_in = stretch_in[0]
    row_pieces = gather_shifts(rows_in, "tp", n_tp)
    full_rows = jnp.zeros((stretch_rows, tensor_width), rows_in.dtype)
    for shift, piece in enumerate(row_pieces):
        source = (tensor_id - shift) % n_tp
        full_rows = lax.dynamic_update_slice_in_dim(full_rows, piece, source * local_width, 1)
    widened = full_rows.astype(jnp.float32)
    mean_square = jnp.mean(widened * widened, axis=1, keepdims=True)
    normed = (widened * lax.rsqrt(mean_square + NORM_EPS) * norm_gain.astype(jnp.float32)).astype(
        jnp.bfloat16
    )

    qkv_cols = w_qkv.shape[1] * w_qkv.shape[2]
    both_weights = jnp.concatenate(
        [w_qkv.reshape(w_qkv.shape[0], qkv_cols), jnp.transpose(w_out)], axis=1
    )
    both_weights = lax.all_gather(both_weights, ("grp", "req"), axis=0, tiled=True)
    weight_piece = both_weights[:, :qkv_cols]
    out_weight_t = both_weights[:, qkv_cols:]
    merged_group = decode_slots(
        block_id, group_id, replica_id, n_req, n_grp, local_heads, head_size, scale_factor,
        prompt_cache, req_count, req_map, prefix_len, slot_query, slot_new_kv,
    )
    normed, merged_group = lax.optimization_barrier((normed, merged_group))

    projected = jnp.dot(normed, weight_piece, preferred_element_type=jnp.float32)
    projected = projected.reshape(stretch_rows, 3, local_heads, head_size)
    query_pos = block_id * stretch_rows + jnp.arange(stretch_rows, dtype=jnp.int32)
    cosine, sine_table = rope_angles(length + query_pos, head_size)
    queries = rotate_pairs(projected[:, 0], cosine, sine_table).astype(jnp.bfloat16)
    new_keys = rotate_pairs(projected[:, 1], cosine, sine_table).astype(jnp.bfloat16)
    new_values = projected[:, 2].astype(jnp.bfloat16)
    fresh_kv = jnp.stack(
        [
            new_keys.reshape(stretch_rows, local_width),
            new_values.reshape(stretch_rows, local_width),
        ],
        axis=0,
    )
    local_kv = jnp.concatenate([prompt_cache[0, 0], fresh_kv], axis=1)
    block_span = cache_rows + stretch_rows

    def attend_rows(carry, kv_piece, source):
        row_peak, totals, accumulated = carry
        piece_rows = kv_piece.shape[1]
        offset = jnp.arange(piece_rows, dtype=jnp.int32)
        from_cache = offset < cache_rows
        cache_pos = source * cache_rows + offset
        stretch_pos = source * stretch_rows + offset - cache_rows
        allowed = jnp.where(
            from_cache[None, :],
            cache_pos[None, :] < length,
            stretch_pos[None, :] <= query_pos[:, None],
        )
        piece_keys = kv_piece[0].reshape(piece_rows, local_heads, head_size)
        piece_values = kv_piece[1].reshape(piece_rows, local_heads, head_size)
        scores = (
            jnp.einsum("qhe,khe->hqk", queries, piece_keys, preferred_element_type=jnp.float32)
            * scale_factor
        )
        key_gate = allowed[None]
        masked = jnp.where(key_gate, scores, NEG_FLOOR)
        new_peak = jnp.maximum(row_peak, jnp.max(masked, axis=2))
        shrink = jnp.exp(row_peak - new_peak)
        weights = jnp.where(key_gate, jnp.exp(masked - new_peak[..., None]), 0.0)
        totals = totals * shrink + jnp.sum(weights, axis=2)
        update = jnp.einsum(
            "hqk,khe->qhe",
            weights.astype(jnp.bfloat16),
            piece_values,
            preferred_element_type=jnp.float32,
        )
        accumulated = accumulated * jnp.transpose(shrink)[:, :, None] + update
        return (new_peak, totals, accumulated)

    state = (
        jnp.full((local_heads, stretch_rows), NEG_FLOOR, jnp.float32),
        jnp.zeros((local_heads, stretch_rows), jnp.float32),
        jnp.zeros((stretch_rows, local_heads, head_size), jnp.float32),
    )
    chip_swap = [(i, i ^ 2) for i in range(n_req)]
    upward = [(i, i ^ 2) for i in range(n_req) if i < (i ^ 2)]
    chunk_rows = stretch_rows // 4
    partner_cache = lax.ppermute(prompt_cache[0, 0], "req", chip_swap)
    partner_fresh = [
        lax.ppermute(fresh_kv[:, c * chunk_rows : (c + 1) * chunk_rows], "req", upward)
        for c in range(4)
    ]
    partner_kv = jnp.concatenate([partner_cache] + partner_fresh, axis=1)
    core_pair = jnp.stack([local_kv, partner_kv], axis=0)
    sibling_kv = lax.ppermute(core_pair, "req", [(i, i ^ 1) for i in range(n_req)])
    state = attend_rows(state, local_kv, block_id)
    remote_kv = jnp.concatenate([partner_kv[None], sibling_kv], axis=0)
    remote_xor = jnp.array([2, 1, 3], dtype=jnp.int32)

    def remote_block(step, inner_state):
        piece = lax.dynamic_index_in_dim(remote_kv, step, 0, keepdims=False)
        return attend_rows(inner_state, piece, jnp.bitwise_xor(block_id, remote_xor[step]))

    state = lax.fori_loop(0, n_req - 1, remote_block, state)
    row_peak, totals, accumulated = state
    attended = (
        (accumulated / jnp.transpose(totals)[:, :, None])
        .astype(jnp.bfloat16)
        .reshape(stretch_rows, local_width)
    )
    branch = None
    for shift in range(n_tp):
        target = (tensor_id + shift) % n_tp
        weight_block = lax.dynamic_slice_in_dim(out_weight_t, target * local_width, local_width, 0)
        product = lax.dot_general(
            attended,
            weight_block,
            (((1,), (1,)), ((), ())),
            preferred_element_type=jnp.float32,
        ).astype(jnp.bfloat16)
        if shift:
            product = lax.ppermute(
                product, "tp", [(i, (i + shift) % n_tp) for i in range(n_tp)]
            )
        if shift == 1:
            product, merged_group = lax.optimization_barrier((product, merged_group))
        term = product.astype(jnp.float32)
        branch = term if branch is None else branch + term
    branch = branch.astype(jnp.bfloat16)
    result = finish_decode(
        merged_group, group_id, replica_id, n_grp, local_heads, head_size, scale_factor,
        prompt_cache, req_count, req_map, slot_query, slot_new_kv,
    )

    return (branch[None], result[None])


def solution(mesh):
    placed = (
        P("grp", "req", "tp"),
        P(),
        P(("grp", "req"), None, "tp"),
        P("tp", ("grp", "req")),
        P("grp", None, None, "req", "tp"),
        P(),
        P(),
        P(),
        P(),
        P(("grp", "req"), None, None, "tp"),
        P(("grp", "req"), None, None, None, "tp"),
    )
    return jax.shard_map(
        per_device,
        mesh=mesh,
        in_specs=placed,
        out_specs=(P("grp", "req", "tp"), P(("grp", "req"), None, None, "tp")),
        check_vma=False,
    )
```
